32 devices in a mesh: grp: 4 (over y, x), dev: 8 (over z, core).
Axes of the slice: x: 2, y: 2, z: 4, core: 2. Of those that a mesh axis runs over, the one named last changes fastest.
Arguments:
- load_vector: bfloat16 [4, 8, 2, 48, 2304], P('grp', 'dev'), may hold values from -6 to 6
- transform: float32 [4, 8, 2, 48, 48], P('grp', 'dev'), may hold values from -0.875 to 0.875
- diagonal: float32 [4, 8, 2, 48], P('grp', 'dev'), may hold values from 0.05 to 4
- scaling: float32 [4, 8, 2, 3], P('grp', 'dev'), may hold values from 0.5 to 2
- live_count: int32 [4, 8], replicated, may hold values from 1 to 2
- coarse_inverse: float32 [4, 8, 6, 48], P('grp', 'dev'), may hold values from -48 to 48, as said below
Outputs:
- multiplier: float32 [4, 8, 2, 3, 2304], P('grp', 'dev')
- residual: float32 [4, 8, 2, 3, 2304], P('grp', 'dev')
The draws below stay inside these ranges and needn't reach their ends.
Inputs may be any that keep to these rules, and one draw needn't show every extreme that they name: Read as 4 matrices of order 48, coarse_inverse is symmetric and positive definite in every group.
All inputs are finite; a program needn't handle non-finite values.
Results may differ from the reference program's by a relative error of at most 0.00055.
Values sent between devices are 32-bit elements; how exact they have to be, the bound alone decides.
No kernel may reach another device: no remote copies, remote signals or barrier semaphores. Data moves between devices by JAX's collectives and lax.ppermute only.
A program may use at most 64 MiB of HBM per device.

```python
import math
import jax
import jax.numpy as jnp
from jax import lax

N = 48
P_DEV = 2
FACE = 2304
GROUPS = 4
OWNERS = 8


def draw_coarse_inverse(key, part):
    coarse_order = OWNERS * P_DEV * 3
    diag_key, off_key = jax.random.split(key)
    log_draws = jax.random.uniform(diag_key, (GROUPS, coarse_order), jnp.float32, math.log(0.5), 0.0)
    diag_vals = N * jnp.exp(log_draws)
    off_bound = 0.475 * N / coarse_order
    raw_draws = jax.random.uniform(off_key, (GROUPS, coarse_order, coarse_order), jnp.float32, -off_bound, off_bound)
    symmetric = 0.5 * (raw_draws + jnp.swapaxes(raw_draws, 1, 2))
    eye_mask = jnp.eye(coarse_order, dtype=jnp.float32)
    full_matrix = symmetric * (1.0 - eye_mask) + eye_mask * diag_vals[:, :, None]
    return full_matrix.reshape(GROUPS, OWNERS, P_DEV * 3, coarse_order)


def set_ends(array, rng, smallest, largest):
    place = [jax.random.randint(jax.random.fold_in(rng, axis), (), 0, length) for axis, length in enumerate(array.shape)]
    main_axis = array.shape.index(max(array.shape))
    next_to = place[:main_axis] + [(place[main_axis] + 1) % array.shape[main_axis]] + place[main_axis + 1:]
    return array.at[tuple(place)].set(smallest).at[tuple(next_to)].set(largest)


def shard_levels(own_key, dims, cuts, least, largest):
    gain, own = 1.0, jax.random.fold_in(own_key, 6)
    for position, parts in cuts:
        draws = jnp.exp(jax.random.uniform(jax.random.fold_in(own, position), (parts,), jnp.float32, least / len(cuts), largest / len(cuts)))
        gain = gain * jnp.repeat(draws, dims[position] // parts).reshape([-1 if axis == position else 1 for axis in range(len(dims))])
    return gain


def scatter_about(own_key, dims, deviation, limit, shards=(), kind=jnp.bfloat16):
    values = deviation * jax.random.normal(own_key, dims, jnp.float32)
    if shards:
        values = values * shard_levels(own_key, dims, shards, -0.22, 0.18)
    return jnp.clip(values, -limit, limit).astype(kind)


def setup_inputs(seed: int = 0) -> dict:
    key_list = jax.random.split(jax.random.key(seed), 7)
    load_vector = scatter_about(key_list[0], (GROUPS, OWNERS, P_DEV, N, FACE), 1.0, 6.0, ((0, 4), (1, 8)))
    transform = scatter_about(key_list[1], (GROUPS, OWNERS, P_DEV, N, N), N ** -0.5, 0.875, ((0, 4), (1, 8)), jnp.float32)
    diagonal = jnp.clip(jnp.exp(math.log(4.0) - 4.3820266 * jax.random.uniform(key_list[2], (GROUPS, OWNERS, P_DEV, N), jnp.float32) ** shard_levels(key_list[2], (GROUPS, OWNERS, P_DEV, N), ((0, 4), (1, 8)), -0.2, 0.2)), 0.05, 4.0)
    scaling = jnp.clip(jnp.exp(math.log(2.0) - 1.3862944 * jax.random.uniform(key_list[3], (GROUPS, OWNERS, P_DEV, 3), jnp.float32) ** shard_levels(key_list[3], (GROUPS, OWNERS, P_DEV, 3), ((0, 4), (1, 8)), -0.2, 0.2)), 0.5, 2.0)
    live_count = set_ends(jax.random.randint(key_list[4], (GROUPS, OWNERS), 1, P_DEV + 1), jax.random.fold_in(key_list[4], 1), 1, P_DEV).astype(jnp.int32)
    coarse_inverse = draw_coarse_inverse(jax.random.fold_in(key_list[6], 71), 0)
    return {"load_vector": load_vector, "transform": transform, "diagonal": diagonal, "scaling": scaling, "live_count": live_count, "coarse_inverse": coarse_inverse}


PRECISE = lax.Precision.HIGHEST


def inverse_diagonal(diagonal):
    return 1.0 / (diagonal[:, None, None] + diagonal[None, :, None] + diagonal[None, None, :])


def spectral(patch_load, transform):
    points = transform.shape[0]
    spatial = patch_load.astype(jnp.float32).reshape(points, points, points)
    moved = jnp.einsum("ai,abc->ibc", transform, spatial, precision=PRECISE)
    moved = jnp.einsum("bj,ibc->ijc", transform, moved, precision=PRECISE)
    return jnp.einsum("ck,ijc->ijk", transform, moved, precision=PRECISE)


def face_spectrum(transform, low_side, high_side):
    points = transform.shape[0]
    planes = jnp.stack([low_side, high_side]).reshape(2, 3, points, points)
    hats = jnp.einsum("bj,edbc,ck->edjk", transform, planes, transform, precision=PRECISE)
    low_row = transform[0]
    high_row = transform[points - 1]
    result = low_row[:, None, None] * hats[0, 0][None] + high_row[:, None, None] * hats[1, 0][None]
    result = result + low_row[None, :, None] * hats[0, 1][:, None, :] + high_row[None, :, None] * hats[1, 1][:, None, :]
    result = result + low_row[None, None, :] * hats[0, 2][:, :, None] + high_row[None, None, :] * hats[1, 2][:, :, None]
    return result


def trace_solved(transform, solved):
    points = transform.shape[0]
    end_rows = jnp.stack([transform[0], transform[points - 1]])
    along_a = jnp.einsum("ei,ijk->ejk", end_rows, solved, precision=PRECISE)
    along_b = jnp.einsum("ej,ijk->eik", end_rows, solved, precision=PRECISE)
    along_c = jnp.einsum("ek,ijk->eij", end_rows, solved, precision=PRECISE)
    planes = jnp.stack([along_a, along_b, along_c], axis=1)
    traces = jnp.einsum("bj,edjk,ck->edbc", transform, planes, transform, precision=PRECISE)
    return traces.reshape(2, 3, points * points)


def setup_patch(patch_load, transform, diagonal):
    return trace_solved(transform, inverse_diagonal(diagonal) * spectral(patch_load, transform))


def apply_patch(transform, diagonal, low_side, high_side):
    return trace_solved(transform, inverse_diagonal(diagonal) * face_spectrum(transform, low_side, high_side))


def reference(load_vector, transform, diagonal, scaling, live_count, coarse_inverse):
    groups, owners, slot_count, points, face_size = load_vector.shape
    devices_all = groups * owners
    flat_transform = transform.reshape(devices_all, slot_count, points, points)
    flat_diagonal = diagonal.reshape(devices_all, slot_count, points)
    traces = lax.map(lambda item: jax.vmap(setup_patch)(*item), (load_vector.reshape(devices_all, slot_count, points, face_size), flat_transform, flat_diagonal))
    traces = traces.reshape(groups, owners, slot_count, 2, 3, face_size)
    slot_index = jnp.arange(slot_count, dtype=jnp.int32)[None, None, :]
    in_use = slot_index < live_count[:, :, None]
    nothing = jnp.zeros_like(in_use[:, :, :1])
    live_x = in_use & jnp.roll(in_use, -1, axis=1)
    live_y = in_use & jnp.roll(in_use, -1, axis=0)
    live_z = in_use & jnp.concatenate([in_use[:, :, 1:], nothing], axis=2)
    alive = jnp.stack([live_x, live_y, live_z], axis=-1).astype(jnp.float32)[..., None]

    def slot_before(vector):
        return jnp.concatenate([jnp.zeros_like(vector[:, :, :1]), vector[:, :, :-1]], axis=2)

    def slot_after(vector):
        return jnp.concatenate([vector[:, :, 1:], jnp.zeros_like(vector[:, :, :1])], axis=2)

    def jumps(traces_now):
        low_side = traces_now[:, :, :, 0]
        high_side = traces_now[:, :, :, 1]
        following = jnp.stack([jnp.roll(low_side[..., 0, :], -1, axis=1), jnp.roll(low_side[..., 1, :], -1, axis=0), slot_after(low_side[..., 2, :])], axis=3)
        return alive * (high_side - following)

    def operate(direction):
        preceding = jnp.stack([jnp.roll(direction[..., 0, :], 1, axis=1), jnp.roll(direction[..., 1, :], 1, axis=0), slot_before(direction[..., 2, :])], axis=3)
        applied = lax.map(lambda item: jax.vmap(apply_patch)(*item), (flat_transform, flat_diagonal, (-preceding).reshape(devices_all, slot_count, 3, face_size), direction.reshape(devices_all, slot_count, 3, face_size)))
        return jumps(applied.reshape(groups, owners, slot_count, 2, 3, face_size))

    coarse_size = owners * slot_count * 3
    matrices = coarse_inverse.reshape(groups, coarse_size, coarse_size)
    weight = scaling[..., None]

    def precondition(vector):
        means = jnp.mean(vector, axis=-1).reshape(groups, coarse_size)
        coarse_vals = jnp.einsum("gkl,gl->gk", matrices, means, precision=PRECISE)
        return weight * vector + alive * coarse_vals.reshape(groups, owners, slot_count, 3, 1)

    jump = jumps(traces)
    multiplier = jnp.zeros_like(jump)
    residual = jump
    direction = precondition(residual)
    product = jnp.sum(residual * direction)
    for iteration in range(2):
        applied = operate(direction)
        step_len = product / jnp.sum(direction * applied)
        multiplier = multiplier + step_len * direction
        residual = residual - step_len * applied
        if iteration == 0:
            precond = precondition(residual)
            new_product = jnp.sum(residual * precond)
            direction = precond + (new_product / product) * direction
            product = new_product
    return multiplier, residual
```

```python
import jax
import jax.numpy as jnp
from jax import lax
from jax.sharding import PartitionSpec as P

PRECISE = lax.Precision.HIGHEST


def shifted(block, axis, distance):
    devices = range(lax.axis_size(axis))
    route = [((i - distance) % len(devices), i) for i in devices]
    return lax.ppermute(block, axis, route)


def inverse_diagonal(diagonal):
    return 1.0 / (diagonal[:, None, None] + diagonal[None, :, None] + diagonal[None, None, :])


def spectral(patch_load, transform):
    points = transform.shape[0]
    spatial = patch_load.astype(jnp.float32).reshape(points, points, points)
    moved = jnp.einsum("ai,abc->ibc", transform, spatial, precision=PRECISE)
    moved = jnp.einsum("bj,ibc->ijc", transform, moved, precision=PRECISE)
    return jnp.einsum("ck,ijc->ijk", transform, moved, precision=PRECISE)


def face_spectrum(transform, low_side, high_side):
    points = transform.shape[0]
    planes = jnp.stack([low_side, high_side]).reshape(2, 3, points, points)
    hats = jnp.einsum("bj,edbc,ck->edjk", transform, planes, transform, precision=PRECISE)
    low_row = transform[0]
    high_row = transform[points - 1]
    result = low_row[:, None, None] * hats[0, 0][None] + high_row[:, None, None] * hats[1, 0][None]
    result = (
        result
        + low_row[None, :, None] * hats[0, 1][:, None, :]
        + high_row[None, :, None] * hats[1, 1][:, None, :]
    )
    result = (
        result
        + low_row[None, None, :] * hats[0, 2][:, :, None]
        + high_row[None, None, :] * hats[1, 2][:, :, None]
    )
    return result


def trace_solved(transform, solved):
    points = transform.shape[0]
    end_rows = jnp.stack([transform[0], transform[points - 1]])
    along_a = jnp.einsum("ei,ijk->ejk", end_rows, solved, precision=PRECISE)
    along_b = jnp.einsum("ej,ijk->eik", end_rows, solved, precision=PRECISE)
    along_c = jnp.einsum("ek,ijk->eij", end_rows, solved, precision=PRECISE)
    planes = jnp.stack([along_a, along_b, along_c], axis=1)
    traces = jnp.einsum("bj,edjk,ck->edbc", transform, planes, transform, precision=PRECISE)
    return traces.reshape(2, 3, points * points)


def setup_one(patch_load, one_transform, one_inverse):
    return trace_solved(one_transform, one_inverse * spectral(patch_load, one_transform))


def apply_one(one_transform, one_inverse, low_side, high_side):
    return trace_solved(
        one_transform, one_inverse * face_spectrum(one_transform, low_side, high_side)
    )


def slot_before(vector):
    return jnp.concatenate([jnp.zeros_like(vector[:1]), vector[:-1]], axis=0)


def slot_after(vector):
    return jnp.concatenate([vector[1:], jnp.zeros_like(vector[:1])], axis=0)


def on_device(load_vector, transform, diagonal, scaling, live_count, coarse_inverse):
    patch_loads = load_vector[0, 0]
    transforms = transform[0, 0]
    diagonals = diagonal[0, 0]
    weights = scaling[0, 0]
    coarse_rows = coarse_inverse[0, 0]
    slot_count = patch_loads.shape[0]
    coarse_size = coarse_rows.shape[-1]
    group_index = lax.axis_index("grp")
    owner_index = lax.axis_index("dev")
    groups = lax.axis_size("grp")
    owners = lax.axis_size("dev")
    prev_owner = (owner_index + owners - 1) % owners
    prev_group = (group_index + groups - 1) % groups

    rows = coarse_rows.reshape(slot_count, 3, coarse_size)
    from_owner = shifted(jnp.concatenate([rows[:, 0], weights[:, 0:1]], axis=1), "dev", 1)
    from_group = shifted(jnp.concatenate([rows[:, 1], weights[:, 1:2]], axis=1), "grp", 1)
    rows_in = jnp.stack([from_owner[:, :coarse_size], from_group[:, :coarse_size]], axis=1)
    weights_in = jnp.stack([from_owner[:, coarse_size], from_group[:, coarse_size]], axis=1)

    slot_index = jnp.arange(slot_count, dtype=jnp.int32)
    in_use = slot_index[None, None, :] < live_count[:, :, None]
    nothing = jnp.zeros_like(in_use[:, :, :1])
    alive = jnp.stack(
        [
            in_use & jnp.roll(in_use, -1, axis=1),
            in_use & jnp.roll(in_use, -1, axis=0),
            in_use & jnp.concatenate([in_use[:, :, 1:], nothing], axis=2),
        ],
        axis=-1,
    ).astype(jnp.float32)
    live_own = alive[group_index, owner_index]
    live_in = jnp.stack(
        [alive[group_index, prev_owner, :, 0], alive[prev_group, owner_index, :, 1]], axis=1
    )

    inverses = jax.vmap(inverse_diagonal)(diagonals)
    solver = jax.vmap(apply_one)

    def gather_all(payload):
        count = groups * owners
        spread = jnp.broadcast_to(payload[None], (count,) + payload.shape)
        got = lax.all_to_all(spread, ("grp", "dev"), 0, 0, tiled=True)
        return got.reshape(groups, owners, -1)

    def face_means(traces):
        return jnp.mean(traces, axis=-1).reshape(-1)

    def interface_means(raw):
        raw = raw.reshape(groups, owners, slot_count, 2, 3)
        low = raw[:, :, :, 0]
        high = raw[:, :, :, 1]
        following = jnp.stack(
            [
                jnp.roll(low[..., 0], -1, axis=1),
                jnp.roll(low[..., 1], -1, axis=0),
                jnp.concatenate([low[:, :, 1:, 2], jnp.zeros_like(low[:, :, :1, 2])], axis=2),
            ],
            axis=-1,
        )
        return (alive * (high - following)).reshape(groups, coarse_size)

    def coarse(means):
        here = means[group_index]
        before = means[prev_group]
        own = jnp.dot(coarse_rows, here, precision=PRECISE).reshape(slot_count, 3)
        first = jnp.dot(rows_in[:, 0], here, precision=PRECISE)
        second = jnp.dot(rows_in[:, 1], before, precision=PRECISE)
        return own, jnp.stack([first, second], axis=1)

    def jumps(traces_now, both):
        low_side = traces_now[:, 0]
        high_side = traces_now[:, 1]
        low_next_owner = shifted(low_side[:, 0], "dev", -1)
        low_next_group = shifted(low_side[:, 1], "grp", -1)
        following = jnp.stack(
            [low_next_owner, low_next_group, slot_after(low_side[:, 2])], axis=1
        )
        own = live_own[..., None] * (high_side - following)
        if not both:
            return own
        high_prev_owner = shifted(high_side[:, 0], "dev", 1)
        high_prev_group = shifted(high_side[:, 1], "grp", 1)
        leading = jnp.stack([high_prev_owner, high_prev_group], axis=1)
        incoming = live_in[..., None] * (leading - low_side[:, :2])
        return own, incoming

    def solve(v_own, v_in):
        preceding = jnp.stack([v_in[:, 0], v_in[:, 1], slot_before(v_own[:, 2])], axis=1)
        return solver(transforms, inverses, -preceding, v_own)

    def split_dot(v_own, v_in, traces_now):
        low_side = traces_now[:, 0]
        high_side = traces_now[:, 1]
        inner = live_own[:, 2, None] * (high_side[:, 2] - slot_after(low_side[:, 2]))
        first = jnp.sum(live_own[:, :2, None] * v_own[:, :2] * high_side[:, :2])
        second = jnp.sum(live_in[..., None] * v_in * low_side[:, :2])
        return first - second + jnp.sum(v_own[:, 2] * inner)

    def precondition(res_own, res_in, c_own, c_in):
        z_own = weights[..., None] * res_own + live_own[..., None] * c_own[..., None]
        z_in = weights_in[..., None] * res_in + live_in[..., None] * c_in[..., None]
        return z_own, z_in

    start_traces = jax.vmap(setup_one)(patch_loads, transforms, inverses)
    gathered = gather_all(face_means(start_traces))
    res_own, res_in = jumps(start_traces, True)
    c_own, c_in = coarse(interface_means(gathered))
    dir_own, dir_in = precondition(res_own, res_in, c_own, c_in)
    rz_part = jnp.sum(res_own * dir_own)

    traces_one = solve(dir_own, dir_in)
    dq_part = split_dot(dir_own, dir_in, traces_one)
    gathered = gather_all(
        jnp.concatenate([face_means(traces_one), jnp.stack([rz_part, dq_part])])
    )
    img_own, img_in = jumps(traces_one, True)
    totals = jnp.sum(gathered[:, :, slot_count * 6 :], axis=(0, 1))
    product = totals[0]
    curve = totals[1]
    step_len = product / curve
    cq_own, cq_in = coarse(interface_means(gathered[:, :, : slot_count * 6]))
    multiplier = step_len * dir_own
    res_own = res_own - step_len * img_own
    res_in = res_in - step_len * img_in
    z_own, z_in = precondition(
        res_own, res_in, c_own - step_len * cq_own, c_in - step_len * cq_in
    )
    new_part = jnp.sum(res_own * z_own)
    zq_part = jnp.sum(z_own * img_own)

    traces_two = solve(z_own, z_in)
    zfz_part = split_dot(z_own, z_in, traces_two)
    dfz_part = split_dot(dir_own, dir_in, traces_two)
    gathered = gather_all(jnp.stack([new_part, zq_part, zfz_part, dfz_part]))
    fz_own = jumps(traces_two, False)
    totals = jnp.sum(gathered, axis=(0, 1))
    new_product = totals[0]
    ratio = new_product / product
    curve_two = totals[2] + ratio * (totals[1] + totals[3]) + ratio * ratio * curve
    step_two = new_product / curve_two
    direction = z_own + ratio * dir_own
    applied = fz_own + ratio * img_own
    multiplier = multiplier + step_two * direction
    residual = res_own - step_two * applied
    return (multiplier[None, None], residual[None, None])


def solution(mesh):
    return jax.shard_map(
        on_device,
        mesh=mesh,
        in_specs=(
            P("grp", "dev", None, None, None),
            P("grp", "dev", None, None, None),
            P("grp", "dev", None, None),
            P("grp", "dev", None, None),
            P(),
            P("grp", "dev", None, None),
        ),
        out_specs=(P("grp", "dev", None, None, None), P("grp", "dev", None, None, None)),
        check_vma=False,
    )
```

```python
import jax
import jax.numpy as jnp
from jax import lax
from jax.sharding import PartitionSpec as P

PRECISE = lax.Precision.HIGHEST


def shifted(block, axis, distance):
    devices = range(lax.axis_size(axis))
    route = [((i - distance) % len(devices), i) for i in devices]
    return lax.ppermute(block, axis, route)


def inverse_diagonal(diagonal):
    return 1.0 / (diagonal[:, None, None] + diagonal[None, :, None] + diagonal[None, None, :])


def spectral(patch_load, transform):
    points = transform.shape[0]
    spatial = patch_load.astype(jnp.float32).reshape(points, points, points)
    moved = jnp.einsum("ai,abc->ibc", transform, spatial, precision=PRECISE)
    moved = jnp.einsum("bj,ibc->ijc", transform, moved, precision=PRECISE)
    return jnp.einsum("ck,ijc->ijk", transform, moved, precision=PRECISE)


def face_spectrum(transform, low_side, high_side):
    points = transform.shape[0]
    planes = jnp.stack([low_side, high_side]).reshape(2, 3, points, points)
    hats = jnp.einsum("bj,edbc,ck->edjk", transform, planes, transform, precision=PRECISE)
    low_row = transform[0]
    high_row = transform[points - 1]
    result = low_row[:, None, None] * hats[0, 0][None] + high_row[:, None, None] * hats[1, 0][None]
    result = (
        result
        + low_row[None, :, None] * hats[0, 1][:, None, :]
        + high_row[None, :, None] * hats[1, 1][:, None, :]
    )
    result = (
        result
        + low_row[None, None, :] * hats[0, 2][:, :, None]
        + high_row[None, None, :] * hats[1, 2][:, :, None]
    )
    return result


def trace_solved(transform, solved):
    points = transform.shape[0]
    end_rows = jnp.stack([transform[0], transform[points - 1]])
    along_a = jnp.sum(end_rows[:, :, None, None] * solved[None], axis=1)
    along_b = jnp.sum(end_rows[:, None, :, None] * solved[None], axis=2)
    along_c = jnp.sum(end_rows[:, None, None, :] * solved[None], axis=3)
    planes = jnp.stack([along_a, along_b, along_c], axis=1)
    traces = jnp.einsum("bj,edjk,ck->edbc", transform, planes, transform, precision=PRECISE)
    return traces.reshape(2, 3, points * points)


def setup_one(patch_load, one_transform, one_inverse):
    return trace_solved(one_transform, one_inverse * spectral(patch_load, one_transform))


def apply_one(one_transform, one_inverse, low_side, high_side):
    return trace_solved(
        one_transform, one_inverse * face_spectrum(one_transform, low_side, high_side)
    )


def slot_before(vector):
    return jnp.concatenate([jnp.zeros_like(vector[:1]), vector[:-1]], axis=0)


def slot_after(vector):
    return jnp.concatenate([vector[1:], jnp.zeros_like(vector[:1])], axis=0)


def on_device(load_vector, transform, diagonal, scaling, live_count, coarse_inverse):
    patch_loads = load_vector[0, 0]
    transforms = transform[0, 0]
    diagonals = diagonal[0, 0]
    weights = scaling[0, 0]
    coarse_rows = coarse_inverse[0, 0]
    slot_count = patch_loads.shape[0]
    coarse_size = coarse_rows.shape[-1]
    group_index = lax.axis_index("grp")
    owner_index = lax.axis_index("dev")
    groups = lax.axis_size("grp")
    owners = lax.axis_size("dev")
    prev_owner = (owner_index + owners - 1) % owners
    prev_group = (group_index + groups - 1) % groups

    rows = coarse_rows.reshape(slot_count, 3, coarse_size)
    extra_owner = jnp.concatenate([rows[:, 0], weights[:, 0:1]], axis=1)
    extra_group = jnp.concatenate([rows[:, 1], weights[:, 1:2]], axis=1)

    slot_index = jnp.arange(slot_count, dtype=jnp.int32)
    in_use = slot_index[None, None, :] < live_count[:, :, None]
    nothing = jnp.zeros_like(in_use[:, :, :1])
    alive = jnp.stack(
        [
            in_use & jnp.roll(in_use, -1, axis=1),
            in_use & jnp.roll(in_use, -1, axis=0),
            in_use & jnp.concatenate([in_use[:, :, 1:], nothing], axis=2),
        ],
        axis=-1,
    ).astype(jnp.float32)
    live_own = alive[group_index, owner_index]
    live_in = jnp.stack(
        [alive[group_index, prev_owner, :, 0], alive[prev_group, owner_index, :, 1]], axis=1
    )

    inverses = jax.vmap(inverse_diagonal)(diagonals)
    solver = jax.vmap(apply_one)

    def gather_all(payload):
        count = groups * owners
        spread = jnp.broadcast_to(payload[None], (count,) + payload.shape)
        got = lax.all_to_all(spread, ("grp", "dev"), 0, 0, tiled=True)
        return got.reshape(groups, owners, -1)

    def face_means(traces):
        return jnp.mean(traces, axis=-1).reshape(-1)

    def interface_means(raw):
        raw = raw.reshape(groups, owners, slot_count, 2, 3)
        low = raw[:, :, :, 0]
        high = raw[:, :, :, 1]
        following = jnp.stack(
            [
                jnp.roll(low[..., 0], -1, axis=1),
                jnp.roll(low[..., 1], -1, axis=0),
                jnp.concatenate([low[:, :, 1:, 2], jnp.zeros_like(low[:, :, :1, 2])], axis=2),
            ],
            axis=-1,
        )
        return (alive * (high - following)).reshape(groups, coarse_size)

    def coarse(means):
        here = means[group_index]
        before = means[prev_group]
        own = jnp.dot(coarse_rows, here, precision=PRECISE).reshape(slot_count, 3)
        first = jnp.dot(rows_in[:, 0], here, precision=PRECISE)
        second = jnp.dot(rows_in[:, 1], before, precision=PRECISE)
        return own, jnp.stack([first, second], axis=1)

    def jumps(traces_now, both, extra=None):
        low_side = traces_now[:, 0]
        high_side = traces_now[:, 1]
        low_next_owner = shifted(low_side[:, 0], "dev", -1)
        low_next_group = shifted(low_side[:, 1], "grp", -1)
        following = jnp.stack(
            [low_next_owner, low_next_group, slot_after(low_side[:, 2])], axis=1
        )
        own = live_own[..., None] * (high_side - following)
        if not both:
            return own
        face_size = high_side.shape[-1]
        high_prev_owner = shifted(
            jnp.concatenate([high_side[:, 0], extra[0]], axis=1), "dev", 1
        )
        high_prev_group = shifted(
            jnp.concatenate([high_side[:, 1], extra[1]], axis=1), "grp", 1
        )
        leading = jnp.stack(
            [high_prev_owner[:, :face_size], high_prev_group[:, :face_size]], axis=1
        )
        incoming = live_in[..., None] * (leading - low_side[:, :2])
        return own, incoming, (high_prev_owner[:, face_size:], high_prev_group[:, face_size:])

    def solve(v_own, v_in):
        preceding = jnp.stack([v_in[:, 0], v_in[:, 1], slot_before(v_own[:, 2])], axis=1)
        return solver(transforms, inverses, -preceding, v_own)

    def split_dot(v_own, v_in, traces_now):
        low_side = traces_now[:, 0]
        high_side = traces_now[:, 1]
        inner = live_own[:, 2, None] * (high_side[:, 2] - slot_after(low_side[:, 2]))
        first = jnp.sum(live_own[:, :2, None] * v_own[:, :2] * high_side[:, :2])
        second = jnp.sum(live_in[..., None] * v_in * low_side[:, :2])
        return first - second + jnp.sum(v_own[:, 2] * inner)

    def precondition(res_own, res_in, c_own, c_in):
        z_own = weights[..., None] * res_own + live_own[..., None] * c_own[..., None]
        z_in = weights_in[..., None] * res_in + live_in[..., None] * c_in[..., None]
        return z_own, z_in

    start_traces = jax.vmap(setup_one)(patch_loads, transforms, inverses)
    gathered = gather_all(face_means(start_traces))
    res_own, res_in, received = jumps(start_traces, True, (extra_owner, extra_group))
    rows_in = jnp.stack([received[0][:, :coarse_size], received[1][:, :coarse_size]], axis=1)
    weights_in = jnp.stack([received[0][:, coarse_size], received[1][:, coarse_size]], axis=1)
    c_own, c_in = coarse(interface_means(gathered))
    dir_own, dir_in = precondition(res_own, res_in, c_own, c_in)
    rz_part = jnp.sum(res_own * dir_own)

    traces_one = solve(dir_own, dir_in)
    dq_part = split_dot(dir_own, dir_in, traces_one)
    gathered = gather_all(
        jnp.concatenate([face_means(traces_one), jnp.stack([rz_part, dq_part])])
    )
    img_own, img_in, _ = jumps(traces_one, True, (extra_owner[:, :0], extra_group[:, :0]))
    totals = jnp.sum(gathered[:, :, slot_count * 6 :], axis=(0, 1))
    product = totals[0]
    curve = totals[1]
    step_len = product / curve
    cq_own, cq_in = coarse(interface_means(gathered[:, :, : slot_count * 6]))
    multiplier = step_len * dir_own
    res_own = res_own - step_len * img_own
    res_in = res_in - step_len * img_in
    z_own, z_in = precondition(
        res_own, res_in, c_own - step_len * cq_own, c_in - step_len * cq_in
    )
    new_part = jnp.sum(res_own * z_own)
    zq_part = jnp.sum(z_own * img_own)

    traces_two = solve(z_own, z_in)
    zfz_part = split_dot(z_own, z_in, traces_two)
    dfz_part = split_dot(dir_own, dir_in, traces_two)
    gathered = gather_all(jnp.stack([new_part, zq_part, zfz_part, dfz_part]))
    fz_own = jumps(traces_two, False)
    totals = jnp.sum(gathered, axis=(0, 1))
    new_product = totals[0]
    ratio = new_product / product
    curve_two = totals[2] + ratio * (totals[1] + totals[3]) + ratio * ratio * curve
    step_two = new_product / curve_two
    direction = z_own + ratio * dir_own
    applied = fz_own + ratio * img_own
    multiplier = multiplier + step_two * direction
    residual = res_own - step_two * applied
    return (multiplier[None, None], residual[None, None])


def solution(mesh):
    return jax.shard_map(
        on_device,
        mesh=mesh,
        in_specs=(
            P("grp", "dev", None, None, None),
            P("grp", "dev", None, None, None),
            P("grp", "dev", None, None),
            P("grp", "dev", None, None),
            P(),
            P("grp", "dev", None, None),
        ),
        out_specs=(P("grp", "dev", None, None, None), P("grp", "dev", None, None, None)),
        check_vma=False,
    )
```

```python
import jax
import jax.numpy as jnp
from jax import lax
from jax.sharding import PartitionSpec as P

PRECISE = lax.Precision.HIGHEST


def shifted(block, axis, distance):
    devices = range(lax.axis_size(axis))
    route = [((i - distance) % len(devices), i) for i in devices]
    return lax.ppermute(block, axis, route)


def inverse_diagonal(diagonal):
    return 1.0 / (diagonal[:, None, None] + diagonal[None, :, None] + diagonal[None, None, :])


def spectral(patch_load, transform):
    points = transform.shape[0]
    spatial = patch_load.astype(jnp.float32).reshape(points, points, points)
    moved = jnp.einsum("ai,abc->ibc", transform, spatial, precision=PRECISE)
    moved = jnp.einsum("bj,ibc->ijc", transform, moved, precision=PRECISE)
    return jnp.einsum("ck,ijc->ijk", transform, moved, precision=PRECISE)


def face_spectrum(transform, low_side, high_side):
    points = transform.shape[0]
    planes = jnp.stack([low_side, high_side]).reshape(2, 3, points, points)
    hats = jnp.einsum("bj,edbc,ck->edjk", transform, planes, transform, precision=PRECISE)
    low_row = transform[0]
    high_row = transform[points - 1]
    result = low_row[:, None, None] * hats[0, 0][None] + high_row[:, None, None] * hats[1, 0][None]
    result = (
        result
        + low_row[None, :, None] * hats[0, 1][:, None, :]
        + high_row[None, :, None] * hats[1, 1][:, None, :]
    )
    result = (
        result
        + low_row[None, None, :] * hats[0, 2][:, :, None]
        + high_row[None, None, :] * hats[1, 2][:, :, None]
    )
    return result


def trace_solved(transform, solved):
    points = transform.shape[0]
    end_rows = jnp.stack([transform[0], transform[points - 1]])
    along_a = jnp.sum(end_rows[:, :, None, None] * solved[None], axis=1)
    along_b = jnp.sum(end_rows[:, None, :, None] * solved[None], axis=2)
    along_c = jnp.sum(end_rows[:, None, None, :] * solved[None], axis=3)
    planes = jnp.stack([along_a, along_b, along_c], axis=1)
    traces = jnp.einsum("bj,edjk,ck->edbc", transform, planes, transform, precision=PRECISE)
    return traces.reshape(2, 3, points * points)


def setup_one(patch_load, one_transform, one_inverse):
    return trace_solved(one_transform, one_inverse * spectral(patch_load, one_transform))


def apply_one(one_transform, one_inverse, low_side, high_side):
    return trace_solved(
        one_transform, one_inverse * face_spectrum(one_transform, low_side, high_side)
    )


def slot_before(vector):
    return jnp.concatenate([jnp.zeros_like(vector[:1]), vector[:-1]], axis=0)


def slot_after(vector):
    return jnp.concatenate([vector[1:], jnp.zeros_like(vector[:1])], axis=0)


def on_device(load_vector, transform, diagonal, scaling, live_count, coarse_inverse):
    patch_loads = load_vector[0, 0]
    transforms = transform[0, 0]
    diagonals = diagonal[0, 0]
    weights = scaling[0, 0]
    coarse_rows = coarse_inverse[0, 0]
    slot_count = patch_loads.shape[0]
    coarse_size = coarse_rows.shape[-1]
    group_index = lax.axis_index("grp")
    owner_index = lax.axis_index("dev")
    groups = lax.axis_size("grp")
    owners = lax.axis_size("dev")
    prev_owner = (owner_index + owners - 1) % owners
    prev_group = (group_index + groups - 1) % groups

    rows = coarse_rows.reshape(slot_count, 3, coarse_size)
    extra_owner = jnp.concatenate([rows[:, 0], weights[:, 0:1]], axis=1)
    extra_group = jnp.concatenate([rows[:, 1], weights[:, 1:2]], axis=1)

    slot_index = jnp.arange(slot_count, dtype=jnp.int32)
    in_use = slot_index[None, None, :] < live_count[:, :, None]
    nothing = jnp.zeros_like(in_use[:, :, :1])
    alive = jnp.stack(
        [
            in_use & jnp.roll(in_use, -1, axis=1),
            in_use & jnp.roll(in_use, -1, axis=0),
            in_use & jnp.concatenate([in_use[:, :, 1:], nothing], axis=2),
        ],
        axis=-1,
    ).astype(jnp.float32)
    live_own = alive[group_index, owner_index]
    live_in = jnp.stack(
        [alive[group_index, prev_owner, :, 0], alive[prev_group, owner_index, :, 1]], axis=1
    )

    inverses = jax.vmap(inverse_diagonal)(diagonals)
    solver = jax.vmap(apply_one)

    def gather_all(payload):
        count = groups * owners
        spread = jnp.broadcast_to(payload[None], (count,) + payload.shape)
        got = lax.all_to_all(spread, ("grp", "dev"), 0, 0, tiled=True)
        return got.reshape(groups, owners, -1)

    def face_means(traces):
        return jnp.mean(traces, axis=-1).reshape(-1)

    def interface_means(raw):
        raw = raw.reshape(groups, owners, slot_count, 2, 3)
        low = raw[:, :, :, 0]
        high = raw[:, :, :, 1]
        following = jnp.stack(
            [
                jnp.roll(low[..., 0], -1, axis=1),
                jnp.roll(low[..., 1], -1, axis=0),
                jnp.concatenate([low[:, :, 1:, 2], jnp.zeros_like(low[:, :, :1, 2])], axis=2),
            ],
            axis=-1,
        )
        return (alive * (high - following)).reshape(groups, coarse_size)

    def coarse(means):
        here = means[group_index]
        before = means[prev_group]
        own = jnp.dot(coarse_rows, here, precision=PRECISE).reshape(slot_count, 3)
        first = jnp.dot(rows_in[:, 0], here, precision=PRECISE)
        second = jnp.dot(rows_in[:, 1], before, precision=PRECISE)
        return own, jnp.stack([first, second], axis=1)

    def jumps(traces_now, both, extra=None):
        low_side = traces_now[:, 0]
        high_side = traces_now[:, 1]
        low_next_owner = shifted(low_side[:, 0], "dev", -1)
        low_next_group = shifted(low_side[:, 1], "grp", -1)
        following = jnp.stack(
            [low_next_owner, low_next_group, slot_after(low_side[:, 2])], axis=1
        )
        own = live_own[..., None] * (high_side - following)
        if not both:
            return own
        face_size = high_side.shape[-1]
        high_prev_owner = shifted(
            jnp.concatenate([high_side[:, 0], extra[0]], axis=1), "dev", 1
        )
        high_prev_group = shifted(
            jnp.concatenate([high_side[:, 1], extra[1]], axis=1), "grp", 1
        )
        leading = jnp.stack(
            [high_prev_owner[:, :face_size], high_prev_group[:, :face_size]], axis=1
        )
        incoming = live_in[..., None] * (leading - low_side[:, :2])
        return own, incoming, (high_prev_owner[:, face_size:], high_prev_group[:, face_size:])

    def solve(v_own, v_in):
        preceding = jnp.stack([v_in[:, 0], v_in[:, 1], slot_before(v_own[:, 2])], axis=1)
        return solver(transforms, inverses, -preceding, v_own)

    def split_terms(v_own, v_in, traces_now):
        low_side = traces_now[:, 0]
        high_side = traces_now[:, 1]
        second = jnp.concatenate(
            [
                live_in[..., None] * v_in * low_side[:, :2],
                (live_own[:, 2, None] * v_own[:, 2] * slot_after(low_side[:, 2]))[:, None],
            ],
            axis=1,
        )
        return live_own[..., None] * v_own * high_side - second

    def partial_sums(terms):
        return jnp.sum(jnp.stack(terms), axis=(1, 2, 3))

    def precondition(res_own, res_in, c_own, c_in):
        z_own = weights[..., None] * res_own + live_own[..., None] * c_own[..., None]
        z_in = weights_in[..., None] * res_in + live_in[..., None] * c_in[..., None]
        return z_own, z_in

    start_traces = jax.vmap(setup_one)(patch_loads, transforms, inverses)
    gathered = gather_all(face_means(start_traces))
    res_own, res_in, received = jumps(start_traces, True, (extra_owner, extra_group))
    rows_in = jnp.stack([received[0][:, :coarse_size], received[1][:, :coarse_size]], axis=1)
    weights_in = jnp.stack([received[0][:, coarse_size], received[1][:, coarse_size]], axis=1)
    c_own, c_in = coarse(interface_means(gathered))
    dir_own, dir_in = precondition(res_own, res_in, c_own, c_in)
    traces_one = solve(dir_own, dir_in)
    parts = partial_sums([res_own * dir_own, split_terms(dir_own, dir_in, traces_one)])
    gathered = gather_all(jnp.concatenate([face_means(traces_one), parts]))
    img_own, img_in, _ = jumps(traces_one, True, (extra_owner[:, :0], extra_group[:, :0]))
    totals = jnp.sum(gathered[:, :, slot_count * 6 :], axis=(0, 1))
    product = totals[0:1]
    curve = totals[1:2]
    step_len = (product / curve)[:, None, None]
    cq_own, cq_in = coarse(interface_means(gathered[:, :, : slot_count * 6]))
    multiplier = step_len * dir_own
    res_own = res_own - step_len * img_own
    res_in = res_in - step_len * img_in
    z_own, z_in = precondition(
        res_own, res_in, c_own - step_len[0] * cq_own, c_in - step_len[0] * cq_in
    )

    traces_two = solve(z_own, z_in)
    parts = partial_sums(
        [
            res_own * z_own,
            z_own * img_own,
            split_terms(z_own, z_in, traces_two),
            split_terms(dir_own, dir_in, traces_two),
        ]
    )
    gathered = gather_all(parts)
    fz_own = jumps(traces_two, False)
    totals = jnp.sum(gathered, axis=(0, 1))
    new_product = totals[0:1]
    ratio = new_product / product
    curve_two = totals[2:3] + ratio * (totals[1:2] + totals[3:4]) + ratio * ratio * curve
    step_two = (new_product / curve_two)[:, None, None]
    ratio = ratio[:, None, None]
    direction = z_own + ratio * dir_own
    applied = fz_own + ratio * img_own
    multiplier = multiplier + step_two * direction
    residual = res_own - step_two * applied
    return (multiplier[None, None], residual[None, None])


def solution(mesh):
    return jax.shard_map(
        on_device,
        mesh=mesh,
        in_specs=(
            P("grp", "dev", None, None, None),
            P("grp", "dev", None, None, None),
            P("grp", "dev", None, None),
            P("grp", "dev", None, None),
            P(),
            P("grp", "dev", None, None),
        ),
        out_specs=(P("grp", "dev", None, None, None), P("grp", "dev", None, None, None)),
        check_vma=False,
    )
```

```python
import jax
import jax.numpy as jnp
from jax import lax
from jax.sharding import PartitionSpec as P

PRECISE = lax.Precision.HIGHEST
FAST = lax.Precision.HIGH


def shifted(block, axis, distance):
    devices = range(lax.axis_size(axis))
    route = [((i - distance) % len(devices), i) for i in devices]
    return lax.ppermute(block, axis, route)


def inverse_diagonal(diagonal):
    return 1.0 / (diagonal[:, None, None] + diagonal[None, :, None] + diagonal[None, None, :])


def spectral(patch_load, transform):
    points = transform.shape[0]
    spatial = patch_load.astype(jnp.float32).reshape(points, points, points)
    moved = jnp.einsum("ai,abc->ibc", transform, spatial, precision=FAST)
    moved = jnp.einsum("bj,ibc->ijc", transform, moved, precision=FAST)
    return jnp.einsum("ck,ijc->ijk", transform, moved, precision=FAST)


def face_spectrum(transform, low_side, high_side):
    points = transform.shape[0]
    planes = jnp.stack([low_side, high_side]).reshape(2, 3, points, points)
    hats = jnp.einsum("bj,edbc,ck->edjk", transform, planes, transform, precision=FAST)
    low_row = transform[0]
    high_row = transform[points - 1]
    result = low_row[:, None, None] * hats[0, 0][None] + high_row[:, None, None] * hats[1, 0][None]
    result = (
        result
        + low_row[None, :, None] * hats[0, 1][:, None, :]
        + high_row[None, :, None] * hats[1, 1][:, None, :]
    )
    result = (
        result
        + low_row[None, None, :] * hats[0, 2][:, :, None]
        + high_row[None, None, :] * hats[1, 2][:, :, None]
    )
    return result


def trace_solved(transform, solved):
    points = transform.shape[0]
    end_rows = jnp.stack([transform[0], transform[points - 1]])
    along_a = jnp.sum(end_rows[:, :, None, None] * solved[None], axis=1)
    along_b = jnp.sum(end_rows[:, None, :, None] * solved[None], axis=2)
    along_c = jnp.sum(end_rows[:, None, None, :] * solved[None], axis=3)
    planes = jnp.stack([along_a, along_b, along_c], axis=1)
    traces = jnp.einsum("bj,edjk,ck->edbc", transform, planes, transform, precision=FAST)
    return traces.reshape(2, 3, points * points)


def setup_one(patch_load, one_transform, one_inverse):
    return trace_solved(one_transform, one_inverse * spectral(patch_load, one_transform))


def apply_one(one_transform, one_inverse, low_side, high_side):
    return trace_solved(
        one_transform, one_inverse * face_spectrum(one_transform, low_side, high_side)
    )


def slot_before(vector):
    return jnp.concatenate([jnp.zeros_like(vector[:1]), vector[:-1]], axis=0)


def slot_after(vector):
    return jnp.concatenate([vector[1:], jnp.zeros_like(vector[:1])], axis=0)


def on_device(load_vector, transform, diagonal, scaling, live_count, coarse_inverse):
    patch_loads = load_vector[0, 0]
    transforms = transform[0, 0]
    diagonals = diagonal[0, 0]
    weights = scaling[0, 0]
    coarse_rows = coarse_inverse[0, 0]
    slot_count = patch_loads.shape[0]
    coarse_size = coarse_rows.shape[-1]
    group_index = lax.axis_index("grp")
    owner_index = lax.axis_index("dev")
    groups = lax.axis_size("grp")
    owners = lax.axis_size("dev")
    prev_owner = (owner_index + owners - 1) % owners
    prev_group = (group_index + groups - 1) % groups

    rows = coarse_rows.reshape(slot_count, 3, coarse_size)
    extra_owner = jnp.concatenate([rows[:, 0], weights[:, 0:1]], axis=1)
    extra_group = jnp.concatenate([rows[:, 1], weights[:, 1:2]], axis=1)

    slot_index = jnp.arange(slot_count, dtype=jnp.int32)
    in_use = slot_index[None, None, :] < live_count[:, :, None]
    nothing = jnp.zeros_like(in_use[:, :, :1])
    alive = jnp.stack(
        [
            in_use & jnp.roll(in_use, -1, axis=1),
            in_use & jnp.roll(in_use, -1, axis=0),
            in_use & jnp.concatenate([in_use[:, :, 1:], nothing], axis=2),
        ],
        axis=-1,
    ).astype(jnp.float32)
    live_own = alive[group_index, owner_index]
    live_in = jnp.stack(
        [alive[group_index, prev_owner, :, 0], alive[prev_group, owner_index, :, 1]], axis=1
    )

    inverses = jax.vmap(inverse_diagonal)(diagonals)
    solver = jax.vmap(apply_one)

    def gather_all(payload):
        count = groups * owners
        spread = jnp.broadcast_to(payload[None], (count,) + payload.shape)
        got = lax.all_to_all(spread, ("grp", "dev"), 0, 0, tiled=True)
        return got.reshape(groups, owners, -1)

    def face_means(traces):
        return jnp.mean(traces, axis=-1).reshape(-1)

    def interface_means(raw):
        raw = raw.reshape(groups, owners, slot_count, 2, 3)
        low = raw[:, :, :, 0]
        high = raw[:, :, :, 1]
        following = jnp.stack(
            [
                jnp.roll(low[..., 0], -1, axis=1),
                jnp.roll(low[..., 1], -1, axis=0),
                jnp.concatenate([low[:, :, 1:, 2], jnp.zeros_like(low[:, :, :1, 2])], axis=2),
            ],
            axis=-1,
        )
        return (alive * (high - following)).reshape(groups, coarse_size)

    def coarse(means):
        here = means[group_index]
        before = means[prev_group]
        own = jnp.dot(coarse_rows, here, precision=PRECISE).reshape(slot_count, 3)
        first = jnp.dot(rows_in[:, 0], here, precision=PRECISE)
        second = jnp.dot(rows_in[:, 1], before, precision=PRECISE)
        return own, jnp.stack([first, second], axis=1)

    def jumps(traces_now, both, extra=None):
        low_side = traces_now[:, 0]
        high_side = traces_now[:, 1]
        low_next_owner = shifted(low_side[:, 0], "dev", -1)
        low_next_group = shifted(low_side[:, 1], "grp", -1)
        following = jnp.stack(
            [low_next_owner, low_next_group, slot_after(low_side[:, 2])], axis=1
        )
        own = live_own[..., None] * (high_side - following)
        if not both:
            return own
        face_size = high_side.shape[-1]
        high_prev_owner = shifted(
            jnp.concatenate([high_side[:, 0], extra[0]], axis=1), "dev", 1
        )
        high_prev_group = shifted(
            jnp.concatenate([high_side[:, 1], extra[1]], axis=1), "grp", 1
        )
        leading = jnp.stack(
            [high_prev_owner[:, :face_size], high_prev_group[:, :face_size]], axis=1
        )
        incoming = live_in[..., None] * (leading - low_side[:, :2])
        return own, incoming, (high_prev_owner[:, face_size:], high_prev_group[:, face_size:])

    def solve(v_own, v_in):
        preceding = jnp.stack([v_in[:, 0], v_in[:, 1], slot_before(v_own[:, 2])], axis=1)
        return solver(transforms, inverses, -preceding, v_own)

    def split_terms(v_own, v_in, traces_now):
        low_side = traces_now[:, 0]
        high_side = traces_now[:, 1]
        second = jnp.concatenate(
            [
                live_in[..., None] * v_in * low_side[:, :2],
                (live_own[:, 2, None] * v_own[:, 2] * slot_after(low_side[:, 2]))[:, None],
            ],
            axis=1,
        )
        return live_own[..., None] * v_own * high_side - second

    def partial_sums(terms):
        return jnp.sum(jnp.stack(terms), axis=(1, 2, 3))

    def precondition(res_own, res_in, c_own, c_in):
        z_own = weights[..., None] * res_own + live_own[..., None] * c_own[..., None]
        z_in = weights_in[..., None] * res_in + live_in[..., None] * c_in[..., None]
        return z_own, z_in

    start_traces = jax.vmap(setup_one)(patch_loads, transforms, inverses)
    gathered = gather_all(face_means(start_traces))
    res_own, res_in, received = jumps(start_traces, True, (extra_owner, extra_group))
    rows_in = jnp.stack([received[0][:, :coarse_size], received[1][:, :coarse_size]], axis=1)
    weights_in = jnp.stack([received[0][:, coarse_size], received[1][:, coarse_size]], axis=1)
    c_own, c_in = coarse(interface_means(gathered))
    dir_own, dir_in = precondition(res_own, res_in, c_own, c_in)
    traces_one = solve(dir_own, dir_in)
    parts = partial_sums([res_own * dir_own, split_terms(dir_own, dir_in, traces_one)])
    gathered = gather_all(jnp.concatenate([face_means(traces_one), parts]))
    img_own, img_in, _ = jumps(traces_one, True, (extra_owner[:, :0], extra_group[:, :0]))
    totals = jnp.sum(gathered[:, :, slot_count * 6 :], axis=(0, 1))
    product = totals[0:1]
    curve = totals[1:2]
    step_len = (product / curve)[:, None, None]
    cq_own, cq_in = coarse(interface_means(gathered[:, :, : slot_count * 6]))
    multiplier = step_len * dir_own
    res_own = res_own - step_len * img_own
    res_in = res_in - step_len * img_in
    z_own, z_in = precondition(
        res_own, res_in, c_own - step_len[0] * cq_own, c_in - step_len[0] * cq_in
    )

    traces_two = solve(z_own, z_in)
    parts = partial_sums(
        [
            res_own * z_own,
            z_own * img_own,
            split_terms(z_own, z_in, traces_two),
            split_terms(dir_own, dir_in, traces_two),
        ]
    )
    gathered = gather_all(parts)
    fz_own = jumps(traces_two, False)
    totals = jnp.sum(gathered, axis=(0, 1))
    new_product = totals[0:1]
    ratio = new_product / product
    curve_two = totals[2:3] + ratio * (totals[1:2] + totals[3:4]) + ratio * ratio * curve
    step_two = (new_product / curve_two)[:, None, None]
    ratio = ratio[:, None, None]
    direction = z_own + ratio * dir_own
    applied = fz_own + ratio * img_own
    multiplier = multiplier + step_two * direction
    residual = res_own - step_two * applied
    return (multiplier[None, None], residual[None, None])


def solution(mesh):
    return jax.shard_map(
        on_device,
        mesh=mesh,
        in_specs=(
            P("grp", "dev", None, None, None),
            P("grp", "dev", None, None, None),
            P("grp", "dev", None, None),
            P("grp", "dev", None, None),
            P(),
            P("grp", "dev", None, None),
        ),
        out_specs=(P("grp", "dev", None, None, None), P("grp", "dev", None, None, None)),
        check_vma=False,
    )
```

```python
import jax
import jax.numpy as jnp
from jax import lax
from jax.sharding import PartitionSpec as P

PRECISE = lax.Precision.HIGHEST
FAST = lax.Precision.HIGH


def shifted(block, axis, distance):
    devices = range(lax.axis_size(axis))
    route = [((i - distance) % len(devices), i) for i in devices]
    return lax.ppermute(block, axis, route)


def inverse_diagonal(diagonal):
    return 1.0 / (diagonal[:, None, None] + diagonal[None, :, None] + diagonal[None, None, :])


def spectral(patch_load, transform):
    points = transform.shape[0]
    spatial = patch_load.astype(jnp.float32).reshape(points, points, points)
    moved = jnp.einsum("ai,abc->ibc", transform, spatial, precision=FAST)
    moved = jnp.einsum("bj,ibc->ijc", transform, moved, precision=FAST)
    return jnp.einsum("ck,ijc->ijk", transform, moved, precision=FAST)


def face_spectrum(transform, low_side, high_side):
    points = transform.shape[0]
    planes = jnp.stack([low_side, high_side]).reshape(2, 3, points, points)
    hats = jnp.einsum("bj,edbc,ck->edjk", transform, planes, transform, precision=FAST)
    low_row = transform[0]
    high_row = transform[points - 1]
    result = low_row[:, None, None] * hats[0, 0][None] + high_row[:, None, None] * hats[1, 0][None]
    result = (
        result
        + low_row[None, :, None] * hats[0, 1][:, None, :]
        + high_row[None, :, None] * hats[1, 1][:, None, :]
    )
    result = (
        result
        + low_row[None, None, :] * hats[0, 2][:, :, None]
        + high_row[None, None, :] * hats[1, 2][:, :, None]
    )
    return result


def trace_solved(transform, solved):
    points = transform.shape[0]
    end_rows = jnp.stack([transform[0], transform[points - 1]])
    along_a = jnp.sum(end_rows[:, :, None, None] * solved[None], axis=1)
    along_b = jnp.sum(end_rows[:, None, :, None] * solved[None], axis=2)
    along_c = jnp.sum(end_rows[:, None, None, :] * solved[None], axis=3)
    planes = jnp.stack([along_a, along_b, along_c], axis=1)
    traces = jnp.einsum("bj,edjk,ck->edbc", transform, planes, transform, precision=FAST)
    return traces.reshape(2, 3, points * points)


def setup_one(patch_load, one_transform, one_inverse):
    return trace_solved(one_transform, one_inverse * spectral(patch_load, one_transform))


def apply_one(one_transform, one_inverse, low_side, high_side):
    return trace_solved(
        one_transform, one_inverse * face_spectrum(one_transform, low_side, high_side)
    )


def slot_before(vector):
    return jnp.concatenate([jnp.zeros_like(vector[:1]), vector[:-1]], axis=0)


def slot_after(vector):
    return jnp.concatenate([vector[1:], jnp.zeros_like(vector[:1])], axis=0)


def on_device(load_vector, transform, diagonal, scaling, live_count, coarse_inverse):
    patch_loads = load_vector[0, 0]
    transforms = transform[0, 0]
    diagonals = diagonal[0, 0]
    weights = scaling[0, 0]
    coarse_rows = coarse_inverse[0, 0]
    slot_count = patch_loads.shape[0]
    coarse_size = coarse_rows.shape[-1]
    group_index = lax.axis_index("grp")
    owner_index = lax.axis_index("dev")
    groups = lax.axis_size("grp")
    owners = lax.axis_size("dev")
    prev_owner = (owner_index + owners - 1) % owners
    prev_group = (group_index + groups - 1) % groups

    rows = coarse_rows.reshape(slot_count, 3, coarse_size)
    extra_owner = jnp.concatenate([rows[:, 0], weights[:, 0:1]], axis=1)
    extra_group = jnp.concatenate([rows[:, 1], weights[:, 1:2]], axis=1)

    slot_index = jnp.arange(slot_count, dtype=jnp.int32)
    in_use = slot_index[None, None, :] < live_count[:, :, None]
    nothing = jnp.zeros_like(in_use[:, :, :1])
    alive = jnp.stack(
        [
            in_use & jnp.roll(in_use, -1, axis=1),
            in_use & jnp.roll(in_use, -1, axis=0),
            in_use & jnp.concatenate([in_use[:, :, 1:], nothing], axis=2),
        ],
        axis=-1,
    ).astype(jnp.float32)
    live_own = alive[group_index, owner_index]
    live_in = jnp.stack(
        [alive[group_index, prev_owner, :, 0], alive[prev_group, owner_index, :, 1]], axis=1
    )

    inverses = jax.vmap(inverse_diagonal)(diagonals)
    solver = jax.vmap(apply_one)

    def gather_all(payload):
        count = groups * owners
        spread = jnp.broadcast_to(payload[None], (count,) + payload.shape)
        got = lax.all_to_all(spread, ("grp", "dev"), 0, 0, tiled=True)
        return got.reshape(groups, owners, -1)

    def face_means(traces):
        return jnp.mean(traces, axis=-1).reshape(-1)

    def interface_means(raw):
        raw = raw.reshape(groups, owners, slot_count, 2, 3)
        low = raw[:, :, :, 0]
        high = raw[:, :, :, 1]
        following = jnp.stack(
            [
                jnp.roll(low[..., 0], -1, axis=1),
                jnp.roll(low[..., 1], -1, axis=0),
                jnp.concatenate([low[:, :, 1:, 2], jnp.zeros_like(low[:, :, :1, 2])], axis=2),
            ],
            axis=-1,
        )
        return (alive * (high - following)).reshape(groups, coarse_size)

    def coarse(means):
        here = means[group_index]
        before = means[prev_group]
        own = jnp.dot(coarse_rows, here, precision=PRECISE).reshape(slot_count, 3)
        first = jnp.dot(rows_in[:, 0], here, precision=PRECISE)
        second = jnp.dot(rows_in[:, 1], before, precision=PRECISE)
        return own, jnp.stack([first, second], axis=1)

    def jumps(traces_now, both, extra=None):
        low_side = traces_now[:, 0]
        high_side = traces_now[:, 1]
        face_size = high_side.shape[-1]
        sends = [low_side[:, 0], low_side[:, 1]]
        if both:
            sends += [
                jnp.concatenate([high_side[:, 0], extra[0]], axis=1),
                jnp.concatenate([high_side[:, 1], extra[1]], axis=1),
            ]
        sends = lax.optimization_barrier(sends)
        low_next_owner = shifted(sends[0], "dev", -1)
        low_next_group = shifted(sends[1], "grp", -1)
        following = jnp.stack(
            [low_next_owner, low_next_group, slot_after(low_side[:, 2])], axis=1
        )
        own = live_own[..., None] * (high_side - following)
        if not both:
            return own
        high_prev_owner = shifted(sends[2], "dev", 1)
        high_prev_group = shifted(sends[3], "grp", 1)
        leading = jnp.stack(
            [high_prev_owner[:, :face_size], high_prev_group[:, :face_size]], axis=1
        )
        incoming = live_in[..., None] * (leading - low_side[:, :2])
        return own, incoming, (high_prev_owner[:, face_size:], high_prev_group[:, face_size:])

    def solve(v_own, v_in):
        preceding = jnp.stack([v_in[:, 0], v_in[:, 1], slot_before(v_own[:, 2])], axis=1)
        return solver(transforms, inverses, -preceding, v_own)

    def split_terms(v_own, v_in, traces_now):
        low_side = traces_now[:, 0]
        high_side = traces_now[:, 1]
        second = jnp.concatenate(
            [
                live_in[..., None] * v_in * low_side[:, :2],
                (live_own[:, 2, None] * v_own[:, 2] * slot_after(low_side[:, 2]))[:, None],
            ],
            axis=1,
        )
        return live_own[..., None] * v_own * high_side - second

    def partial_sums(terms):
        return jnp.sum(jnp.stack(terms), axis=(1, 2, 3))

    def precondition(res_own, res_in, c_own, c_in):
        z_own = weights[..., None] * res_own + live_own[..., None] * c_own[..., None]
        z_in = weights_in[..., None] * res_in + live_in[..., None] * c_in[..., None]
        return z_own, z_in

    start_traces = jax.vmap(setup_one)(patch_loads, transforms, inverses)
    gathered = gather_all(face_means(start_traces))
    res_own, res_in, received = jumps(start_traces, True, (extra_owner, extra_group))
    rows_in = jnp.stack([received[0][:, :coarse_size], received[1][:, :coarse_size]], axis=1)
    weights_in = jnp.stack([received[0][:, coarse_size], received[1][:, coarse_size]], axis=1)
    c_own, c_in = coarse(interface_means(gathered))
    dir_own, dir_in = precondition(res_own, res_in, c_own, c_in)
    traces_one = solve(dir_own, dir_in)
    parts = partial_sums([res_own * dir_own, split_terms(dir_own, dir_in, traces_one)])
    gathered = gather_all(jnp.concatenate([face_means(traces_one), parts]))
    img_own, img_in, _ = jumps(traces_one, True, (extra_owner[:, :0], extra_group[:, :0]))
    totals = jnp.sum(gathered[:, :, slot_count * 6 :], axis=(0, 1))
    product = totals[0:1]
    curve = totals[1:2]
    step_len = (product / curve)[:, None, None]
    cq_own, cq_in = coarse(interface_means(gathered[:, :, : slot_count * 6]))
    multiplier = step_len * dir_own
    res_own = res_own - step_len * img_own
    res_in = res_in - step_len * img_in
    z_own, z_in = precondition(
        res_own, res_in, c_own - step_len[0] * cq_own, c_in - step_len[0] * cq_in
    )

    traces_two = solve(z_own, z_in)
    parts = partial_sums(
        [
            res_own * z_own,
            z_own * img_own,
            split_terms(z_own, z_in, traces_two),
            split_terms(dir_own, dir_in, traces_two),
        ]
    )
    gathered = gather_all(parts)
    fz_own = jumps(traces_two, False)
    totals = jnp.sum(gathered, axis=(0, 1))
    new_product = totals[0:1]
    ratio = new_product / product
    curve_two = totals[2:3] + ratio * (totals[1:2] + totals[3:4]) + ratio * ratio * curve
    step_two = (new_product / curve_two)[:, None, None]
    ratio = ratio[:, None, None]
    direction = z_own + ratio * dir_own
    applied = fz_own + ratio * img_own
    multiplier = multiplier + step_two * direction
    residual = res_own - step_two * applied
    return (multiplier[None, None], residual[None, None])


def solution(mesh):
    return jax.shard_map(
        on_device,
        mesh=mesh,
        in_specs=(
            P("grp", "dev", None, None, None),
            P("grp", "dev", None, None, None),
            P("grp", "dev", None, None),
            P("grp", "dev", None, None),
            P(),
            P("grp", "dev", None, None),
        ),
        out_specs=(P("grp", "dev", None, None, None), P("grp", "dev", None, None, None)),
        check_vma=False,
    )
```

```python
import jax
import jax.numpy as jnp
from jax import lax
from jax.sharding import PartitionSpec as P

PRECISE = lax.Precision.HIGHEST
FAST = lax.Precision.HIGH


def shifted(block, axis, distance):
    devices = range(lax.axis_size(axis))
    route = [((i - distance) % len(devices), i) for i in devices]
    return lax.ppermute(block, axis, route)


def inverse_diagonal(diagonal):
    return 1.0 / (diagonal[:, None, None] + diagonal[None, :, None] + diagonal[None, None, :])


def spectral(patch_load, transform):
    points = transform.shape[0]
    spatial = patch_load.astype(jnp.float32).reshape(points, points, points)
    moved = jnp.einsum("ai,abc->ibc", transform, spatial, precision=FAST)
    moved = jnp.einsum("bj,ibc->ijc", transform, moved, precision=FAST)
    return jnp.einsum("ck,ijc->ijk", transform, moved, precision=FAST)


def expansions(transform):
    points = transform.shape[0]
    eye = jnp.eye(points, dtype=transform.dtype)
    ends = [transform[0], transform[points - 1]]
    across = [jnp.kron(row[None, :], eye) for row in ends]
    along = [jnp.kron(eye, row[None, :]) for row in ends]
    return jnp.stack(across + along)


def flat_traces(transform, expand, solved):
    points = transform.shape[0]
    end_rows = jnp.stack([transform[0], transform[points - 1]])
    along_a = jnp.dot(end_rows, solved, precision=FAST).reshape(2, points, points)
    along_b = jnp.einsum("ix,ekx->eik", solved, expand[:2], precision=FAST)
    along_c = jnp.einsum("ix,ejx->eij", solved, expand[2:], precision=FAST)
    planes = jnp.stack([along_a, along_b, along_c], axis=1)
    traces = jnp.einsum("bj,edjk,ck->edbc", transform, planes, transform, precision=FAST)
    return traces.reshape(2, 3, points * points)


def setup_one(patch_load, one_transform, one_inverse, expand):
    points = one_transform.shape[0]
    solved = (one_inverse * spectral(patch_load, one_transform)).reshape(points, points * points)
    return flat_traces(one_transform, expand, solved)


def apply_one(one_transform, one_inverse, expand, low_side, high_side):
    points = one_transform.shape[0]
    planes = jnp.stack([low_side, high_side]).reshape(2, 3, points, points)
    hats = jnp.einsum("bj,edbc,ck->edjk", one_transform, planes, one_transform, precision=FAST)
    end_rows = jnp.stack([one_transform[0], one_transform[points - 1]])
    result = jnp.dot(end_rows.T, hats[:, 0].reshape(2, points * points), precision=FAST)
    mixed = jnp.concatenate([hats[0, 1], hats[1, 1], hats[0, 2], hats[1, 2]], axis=1)
    result = result + jnp.dot(mixed, expand.reshape(-1, points * points), precision=FAST)
    solved = one_inverse.reshape(points, points * points) * result
    return flat_traces(one_transform, expand, solved)


def slot_before(vector):
    return jnp.concatenate([jnp.zeros_like(vector[:1]), vector[:-1]], axis=0)


def slot_after(vector):
    return jnp.concatenate([vector[1:], jnp.zeros_like(vector[:1])], axis=0)


def on_device(load_vector, transform, diagonal, scaling, live_count, coarse_inverse):
    patch_loads = load_vector[0, 0]
    transforms = transform[0, 0]
    diagonals = diagonal[0, 0]
    weights = scaling[0, 0]
    coarse_rows = coarse_inverse[0, 0]
    slot_count = patch_loads.shape[0]
    coarse_size = coarse_rows.shape[-1]
    group_index = lax.axis_index("grp")
    owner_index = lax.axis_index("dev")
    groups = lax.axis_size("grp")
    owners = lax.axis_size("dev")
    prev_owner = (owner_index + owners - 1) % owners
    prev_group = (group_index + groups - 1) % groups

    rows = coarse_rows.reshape(slot_count, 3, coarse_size)
    extra_owner = jnp.concatenate([rows[:, 0], weights[:, 0:1]], axis=1)
    extra_group = jnp.concatenate([rows[:, 1], weights[:, 1:2]], axis=1)

    slot_index = jnp.arange(slot_count, dtype=jnp.int32)
    in_use = slot_index[None, None, :] < live_count[:, :, None]
    nothing = jnp.zeros_like(in_use[:, :, :1])
    alive = jnp.stack(
        [
            in_use & jnp.roll(in_use, -1, axis=1),
            in_use & jnp.roll(in_use, -1, axis=0),
            in_use & jnp.concatenate([in_use[:, :, 1:], nothing], axis=2),
        ],
        axis=-1,
    ).astype(jnp.float32)
    live_own = alive[group_index, owner_index]
    live_in = jnp.stack(
        [alive[group_index, prev_owner, :, 0], alive[prev_group, owner_index, :, 1]], axis=1
    )

    inverses = jax.vmap(inverse_diagonal)(diagonals)
    expands = jax.vmap(expansions)(transforms)
    solver = jax.vmap(apply_one)

    def gather_all(payload):
        count = groups * owners
        spread = jnp.broadcast_to(payload[None], (count,) + payload.shape)
        got = lax.all_to_all(spread, ("grp", "dev"), 0, 0, tiled=True)
        return got.reshape(groups, owners, -1)

    def face_means(traces):
        return jnp.mean(traces, axis=-1).reshape(-1)

    def interface_means(raw):
        raw = raw.reshape(groups, owners, slot_count, 2, 3)
        low = raw[:, :, :, 0]
        high = raw[:, :, :, 1]
        following = jnp.stack(
            [
                jnp.roll(low[..., 0], -1, axis=1),
                jnp.roll(low[..., 1], -1, axis=0),
                jnp.concatenate([low[:, :, 1:, 2], jnp.zeros_like(low[:, :, :1, 2])], axis=2),
            ],
            axis=-1,
        )
        return (alive * (high - following)).reshape(groups, coarse_size)

    def coarse(means):
        here = means[group_index]
        before = means[prev_group]
        own = jnp.dot(coarse_rows, here, precision=PRECISE).reshape(slot_count, 3)
        first = jnp.dot(rows_in[:, 0], here, precision=PRECISE)
        second = jnp.dot(rows_in[:, 1], before, precision=PRECISE)
        return own, jnp.stack([first, second], axis=1)

    def jumps(traces_now, both, extra=None):
        low_side = traces_now[:, 0]
        high_side = traces_now[:, 1]
        face_size = high_side.shape[-1]
        sends = [low_side[:, 0], low_side[:, 1]]
        if both:
            sends += [
                jnp.concatenate([high_side[:, 0], extra[0]], axis=1),
                jnp.concatenate([high_side[:, 1], extra[1]], axis=1),
            ]
        sends = lax.optimization_barrier(sends)
        low_next_owner = shifted(sends[0], "dev", -1)
        low_next_group = shifted(sends[1], "grp", -1)
        following = jnp.stack(
            [low_next_owner, low_next_group, slot_after(low_side[:, 2])], axis=1
        )
        own = live_own[..., None] * (high_side - following)
        if not both:
            return own
        high_prev_owner = shifted(sends[2], "dev", 1)
        high_prev_group = shifted(sends[3], "grp", 1)
        leading = jnp.stack(
            [high_prev_owner[:, :face_size], high_prev_group[:, :face_size]], axis=1
        )
        incoming = live_in[..., None] * (leading - low_side[:, :2])
        return own, incoming, (high_prev_owner[:, face_size:], high_prev_group[:, face_size:])

    def solve(v_own, v_in):
        preceding = jnp.stack([v_in[:, 0], v_in[:, 1], slot_before(v_own[:, 2])], axis=1)
        return solver(transforms, inverses, expands, -preceding, v_own)

    def split_terms(v_own, v_in, traces_now):
        low_side = traces_now[:, 0]
        high_side = traces_now[:, 1]
        second = jnp.concatenate(
            [
                live_in[..., None] * v_in * low_side[:, :2],
                (live_own[:, 2, None] * v_own[:, 2] * slot_after(low_side[:, 2]))[:, None],
            ],
            axis=1,
        )
        return live_own[..., None] * v_own * high_side - second

    def partial_sums(terms):
        return jnp.sum(jnp.stack(terms), axis=(1, 2, 3))

    def precondition(res_own, res_in, c_own, c_in):
        z_own = weights[..., None] * res_own + live_own[..., None] * c_own[..., None]
        z_in = weights_in[..., None] * res_in + live_in[..., None] * c_in[..., None]
        return z_own, z_in

    start_traces = jax.vmap(setup_one)(patch_loads, transforms, inverses, expands)
    gathered = gather_all(face_means(start_traces))
    res_own, res_in, received = jumps(start_traces, True, (extra_owner, extra_group))
    rows_in = jnp.stack([received[0][:, :coarse_size], received[1][:, :coarse_size]], axis=1)
    weights_in = jnp.stack([received[0][:, coarse_size], received[1][:, coarse_size]], axis=1)
    c_own, c_in = coarse(interface_means(gathered))
    dir_own, dir_in = precondition(res_own, res_in, c_own, c_in)
    traces_one = solve(dir_own, dir_in)
    parts = partial_sums([res_own * dir_own, split_terms(dir_own, dir_in, traces_one)])
    gathered = gather_all(jnp.concatenate([face_means(traces_one), parts]))
    img_own, img_in, _ = jumps(traces_one, True, (extra_owner[:, :0], extra_group[:, :0]))
    totals = jnp.sum(gathered[:, :, slot_count * 6 :], axis=(0, 1))
    product = totals[0:1]
    curve = totals[1:2]
    step_len = (product / curve)[:, None, None]
    cq_own, cq_in = coarse(interface_means(gathered[:, :, : slot_count * 6]))
    multiplier = step_len * dir_own
    res_own = res_own - step_len * img_own
    res_in = res_in - step_len * img_in
    z_own, z_in = precondition(
        res_own, res_in, c_own - step_len[0] * cq_own, c_in - step_len[0] * cq_in
    )

    traces_two = solve(z_own, z_in)
    parts = partial_sums(
        [
            res_own * z_own,
            z_own * img_own,
            split_terms(z_own, z_in, traces_two),
            split_terms(dir_own, dir_in, traces_two),
        ]
    )
    gathered = gather_all(parts)
    fz_own = jumps(traces_two, False)
    totals = jnp.sum(gathered, axis=(0, 1))
    new_product = totals[0:1]
    ratio = new_product / product
    curve_two = totals[2:3] + ratio * (totals[1:2] + totals[3:4]) + ratio * ratio * curve
    step_two = (new_product / curve_two)[:, None, None]
    ratio = ratio[:, None, None]
    direction = z_own + ratio * dir_own
    applied = fz_own + ratio * img_own
    multiplier = multiplier + step_two * direction
    residual = res_own - step_two * applied
    return (multiplier[None, None], residual[None, None])


def solution(mesh):
    return jax.shard_map(
        on_device,
        mesh=mesh,
        in_specs=(
            P("grp", "dev", None, None, None),
            P("grp", "dev", None, None, None),
            P("grp", "dev", None, None),
            P("grp", "dev", None, None),
            P(),
            P("grp", "dev", None, None),
        ),
        out_specs=(P("grp", "dev", None, None, None), P("grp", "dev", None, None, None)),
        check_vma=False,
    )
```

```python
import jax
import jax.numpy as jnp
from jax import lax
from jax.sharding import PartitionSpec as P

PRECISE = lax.Precision.HIGHEST
FAST = lax.Precision.HIGH


def shifted(block, axis, distance):
    devices = range(lax.axis_size(axis))
    route = [((i - distance) % len(devices), i) for i in devices]
    return lax.ppermute(block, axis, route)


def inverse_diagonal(diagonal):
    return 1.0 / (diagonal[:, None, None] + diagonal[None, :, None] + diagonal[None, None, :])


def spectral(patch_load, transform):
    points = transform.shape[0]
    flat = jnp.dot(transform.T, patch_load.astype(jnp.float32), precision=FAST)
    moved = flat.reshape(points, points, points)
    moved = jnp.einsum("bj,ibc->ijc", transform, moved, precision=FAST)
    return jnp.einsum("ck,ijc->ijk", transform, moved, precision=FAST)


def face_spectrum(transform, low_side, high_side):
    points = transform.shape[0]
    planes = jnp.stack([low_side, high_side]).reshape(2, 3, points, points)
    hats = jnp.einsum("bj,edbc,ck->edjk", transform, planes, transform, precision=FAST)
    low_row = transform[0]
    high_row = transform[points - 1]
    result = low_row[:, None, None] * hats[0, 0][None] + high_row[:, None, None] * hats[1, 0][None]
    result = (
        result
        + low_row[None, :, None] * hats[0, 1][:, None, :]
        + high_row[None, :, None] * hats[1, 1][:, None, :]
    )
    result = (
        result
        + low_row[None, None, :] * hats[0, 2][:, :, None]
        + high_row[None, None, :] * hats[1, 2][:, :, None]
    )
    return result


def trace_solved(transform, solved):
    points = transform.shape[0]
    end_rows = jnp.stack([transform[0], transform[points - 1]])
    along_a = jnp.sum(end_rows[:, :, None, None] * solved[None], axis=1)
    along_b = jnp.sum(end_rows[:, None, :, None] * solved[None], axis=2)
    along_c = jnp.sum(end_rows[:, None, None, :] * solved[None], axis=3)
    planes = jnp.stack([along_a, along_b, along_c], axis=1)
    traces = jnp.einsum("bj,edjk,ck->edbc", transform, planes, transform, precision=FAST)
    return traces.reshape(2, 3, points * points)


def setup_one(patch_load, one_transform, one_inverse):
    return trace_solved(one_transform, one_inverse * spectral(patch_load, one_transform))


def apply_one(one_transform, one_inverse, low_side, high_side):
    return trace_solved(
        one_transform, one_inverse * face_spectrum(one_transform, low_side, high_side)
    )


def slot_before(vector):
    return jnp.concatenate([jnp.zeros_like(vector[:1]), vector[:-1]], axis=0)


def slot_after(vector):
    return jnp.concatenate([vector[1:], jnp.zeros_like(vector[:1])], axis=0)


def on_device(load_vector, transform, diagonal, scaling, live_count, coarse_inverse):
    patch_loads = load_vector[0, 0]
    transforms = transform[0, 0]
    diagonals = diagonal[0, 0]
    weights = scaling[0, 0]
    coarse_rows = coarse_inverse[0, 0]
    slot_count = patch_loads.shape[0]
    coarse_size = coarse_rows.shape[-1]
    group_index = lax.axis_index("grp")
    owner_index = lax.axis_index("dev")
    groups = lax.axis_size("grp")
    owners = lax.axis_size("dev")
    prev_owner = (owner_index + owners - 1) % owners
    prev_group = (group_index + groups - 1) % groups

    rows = coarse_rows.reshape(slot_count, 3, coarse_size)
    extra_owner = jnp.concatenate([rows[:, 0], weights[:, 0:1]], axis=1)
    extra_group = jnp.concatenate([rows[:, 1], weights[:, 1:2]], axis=1)

    slot_index = jnp.arange(slot_count, dtype=jnp.int32)
    in_use = slot_index[None, None, :] < live_count[:, :, None]
    nothing = jnp.zeros_like(in_use[:, :, :1])
    alive = jnp.stack(
        [
            in_use & jnp.roll(in_use, -1, axis=1),
            in_use & jnp.roll(in_use, -1, axis=0),
            in_use & jnp.concatenate([in_use[:, :, 1:], nothing], axis=2),
        ],
        axis=-1,
    ).astype(jnp.float32)
    live_own = alive[group_index, owner_index]
    live_in = jnp.stack(
        [alive[group_index, prev_owner, :, 0], alive[prev_group, owner_index, :, 1]], axis=1
    )

    inverses = jax.vmap(inverse_diagonal)(diagonals)
    solver = jax.vmap(apply_one)

    def gather_all(payload):
        count = groups * owners
        spread = jnp.broadcast_to(payload[None], (count,) + payload.shape)
        got = lax.all_to_all(spread, ("grp", "dev"), 0, 0, tiled=True)
        return got.reshape(groups, owners, -1)

    def face_means(traces):
        return jnp.mean(traces, axis=-1).reshape(-1)

    def interface_means(raw):
        raw = raw.reshape(groups, owners, slot_count, 2, 3)
        low = raw[:, :, :, 0]
        high = raw[:, :, :, 1]
        following = jnp.stack(
            [
                jnp.roll(low[..., 0], -1, axis=1),
                jnp.roll(low[..., 1], -1, axis=0),
                jnp.concatenate([low[:, :, 1:, 2], jnp.zeros_like(low[:, :, :1, 2])], axis=2),
            ],
            axis=-1,
        )
        return (alive * (high - following)).reshape(groups, coarse_size)

    def coarse(means):
        here = means[group_index]
        before = means[prev_group]
        near = jnp.concatenate([coarse_rows, rows_in[:, 0]], axis=0)
        values = jnp.sum(near * here[None, :], axis=1)
        second = jnp.sum(rows_in[:, 1] * before[None, :], axis=1)
        own = values[: slot_count * 3].reshape(slot_count, 3)
        return own, jnp.stack([values[slot_count * 3 :], second], axis=1)

    def jumps(traces_now, both, extra=None):
        low_side = traces_now[:, 0]
        high_side = traces_now[:, 1]
        face_size = high_side.shape[-1]
        sends = [low_side[:, 0], low_side[:, 1]]
        if both:
            sends += [
                jnp.concatenate([high_side[:, 0], extra[0]], axis=1),
                jnp.concatenate([high_side[:, 1], extra[1]], axis=1),
            ]
        sends = lax.optimization_barrier(sends)
        low_next_owner = shifted(sends[0], "dev", -1)
        low_next_group = shifted(sends[1], "grp", -1)
        following = jnp.stack(
            [low_next_owner, low_next_group, slot_after(low_side[:, 2])], axis=1
        )
        own = live_own[..., None] * (high_side - following)
        if not both:
            return own
        high_prev_owner = shifted(sends[2], "dev", 1)
        high_prev_group = shifted(sends[3], "grp", 1)
        leading = jnp.stack(
            [high_prev_owner[:, :face_size], high_prev_group[:, :face_size]], axis=1
        )
        incoming = live_in[..., None] * (leading - low_side[:, :2])
        return own, incoming, (high_prev_owner[:, face_size:], high_prev_group[:, face_size:])

    def solve(v_own, v_in):
        preceding = jnp.stack([v_in[:, 0], v_in[:, 1], slot_before(v_own[:, 2])], axis=1)
        return solver(transforms, inverses, -preceding, v_own)

    def split_terms(v_own, v_in, traces_now):
        low_side = traces_now[:, 0]
        high_side = traces_now[:, 1]
        second = jnp.concatenate(
            [
                live_in[..., None] * v_in * low_side[:, :2],
                (live_own[:, 2, None] * v_own[:, 2] * slot_after(low_side[:, 2]))[:, None],
            ],
            axis=1,
        )
        return live_own[..., None] * v_own * high_side - second

    def partial_sums(terms):
        return jnp.sum(jnp.stack(terms), axis=(1, 2, 3))

    def precondition(res_own, res_in, c_own, c_in):
        z_own = weights[..., None] * res_own + live_own[..., None] * c_own[..., None]
        z_in = weights_in[..., None] * res_in + live_in[..., None] * c_in[..., None]
        return z_own, z_in

    start_traces = jax.vmap(setup_one)(patch_loads, transforms, inverses)
    gathered = gather_all(face_means(start_traces))
    res_own, res_in, received = jumps(start_traces, True, (extra_owner, extra_group))
    rows_in = jnp.stack([received[0][:, :coarse_size], received[1][:, :coarse_size]], axis=1)
    weights_in = jnp.stack([received[0][:, coarse_size], received[1][:, coarse_size]], axis=1)
    c_own, c_in = coarse(interface_means(gathered))
    dir_own, dir_in = precondition(res_own, res_in, c_own, c_in)
    traces_one = solve(dir_own, dir_in)
    parts = partial_sums([res_own * dir_own, split_terms(dir_own, dir_in, traces_one)])
    gathered = gather_all(jnp.concatenate([face_means(traces_one), parts]))
    img_own, img_in, _ = jumps(traces_one, True, (extra_owner[:, :0], extra_group[:, :0]))
    totals = jnp.sum(gathered[:, :, slot_count * 6 :], axis=(0, 1))
    product = totals[0:1]
    curve = totals[1:2]
    step_len = (product / curve)[:, None, None]
    cq_own, cq_in = coarse(interface_means(gathered[:, :, : slot_count * 6]))
    multiplier = step_len * dir_own
    res_own = res_own - step_len * img_own
    res_in = res_in - step_len * img_in
    z_own, z_in = precondition(
        res_own, res_in, c_own - step_len[0] * cq_own, c_in - step_len[0] * cq_in
    )

    traces_two = solve(z_own, z_in)
    parts = partial_sums(
        [
            res_own * z_own,
            z_own * img_own,
            split_terms(z_own, z_in, traces_two),
            split_terms(dir_own, dir_in, traces_two),
        ]
    )
    gathered = gather_all(parts)
    fz_own = jumps(traces_two, False)
    totals = jnp.sum(gathered, axis=(0, 1))
    new_product = totals[0:1]
    ratio = new_product / product
    curve_two = totals[2:3] + ratio * (totals[1:2] + totals[3:4]) + ratio * ratio * curve
    step_two = (new_product / curve_two)[:, None, None]
    ratio = ratio[:, None, None]
    direction = z_own + ratio * dir_own
    applied = fz_own + ratio * img_own
    multiplier = multiplier + step_two * direction
    residual = res_own - step_two * applied
    return (multiplier[None, None], residual[None, None])


def solution(mesh):
    return jax.shard_map(
        on_device,
        mesh=mesh,
        in_specs=(
            P("grp", "dev", None, None, None),
            P("grp", "dev", None, None, None),
            P("grp", "dev", None, None),
            P("grp", "dev", None, None),
            P(),
            P("grp", "dev", None, None),
        ),
        out_specs=(P("grp", "dev", None, None, None), P("grp", "dev", None, None, None)),
        check_vma=False,
    )
```

```python
import jax
import jax.numpy as jnp
from jax import lax
from jax.sharding import PartitionSpec as P

PRECISE = lax.Precision.HIGHEST
FAST = lax.Precision.HIGH


def shifted(block, axis, distance):
    devices = range(lax.axis_size(axis))
    route = [((i - distance) % len(devices), i) for i in devices]
    return lax.ppermute(block, axis, route)


def inverse_diagonal(diagonal):
    return 1.0 / (diagonal[:, None, None] + diagonal[None, :, None] + diagonal[None, None, :])


def spectral(patch_load, transform):
    points = transform.shape[0]
    spatial = patch_load.astype(jnp.float32).reshape(points, points, points)
    moved = jnp.einsum("ai,abc->ibc", transform, spatial, precision=FAST)
    moved = jnp.einsum("bj,ibc->ijc", transform, moved, precision=FAST)
    return jnp.einsum("ck,ijc->ijk", transform, moved, precision=FAST)


def face_spectrum(transform, low_side, high_side):
    points = transform.shape[0]
    planes = jnp.stack([low_side, high_side]).reshape(2, 3, points, points)
    hats = jnp.einsum("bj,edbc,ck->edjk", transform, planes, transform, precision=FAST)
    low_row = transform[0]
    high_row = transform[points - 1]
    result = low_row[:, None, None] * hats[0, 0][None] + high_row[:, None, None] * hats[1, 0][None]
    result = (
        result
        + low_row[None, :, None] * hats[0, 1][:, None, :]
        + high_row[None, :, None] * hats[1, 1][:, None, :]
    )
    result = (
        result
        + low_row[None, None, :] * hats[0, 2][:, :, None]
        + high_row[None, None, :] * hats[1, 2][:, :, None]
    )
    return result


def trace_solved(transform, solved):
    points = transform.shape[0]
    end_rows = jnp.stack([transform[0], transform[points - 1]])
    along_a = jnp.sum(end_rows[:, :, None, None] * solved[None], axis=1)
    along_b = jnp.sum(end_rows[:, None, :, None] * solved[None], axis=2)
    along_c = jnp.sum(end_rows[:, None, None, :] * solved[None], axis=3)
    planes = jnp.stack([along_a, along_b, along_c], axis=1)
    traces = jnp.einsum("bj,edjk,ck->edbc", transform, planes, transform, precision=FAST)
    return traces.reshape(2, 3, points * points)


def setup_one(patch_load, one_transform, one_inverse):
    return trace_solved(one_transform, one_inverse * spectral(patch_load, one_transform))


def apply_one(one_transform, one_inverse, low_side, high_side):
    return trace_solved(
        one_transform, one_inverse * face_spectrum(one_transform, low_side, high_side)
    )


def side_by_side(blocks):
    return jnp.concatenate([blocks[0], blocks[1]], axis=-1)


def solve_pair(transforms, wide_inverse, low_side, high_side):
    slots, points = transforms.shape[0], transforms.shape[1]
    planes = jnp.stack([low_side, high_side], axis=1).reshape(slots, 2, 3, points, points)
    hats = jnp.einsum(
        "sbj,sedbc,sck->sedjk", transforms, planes, transforms, precision=FAST
    )
    ends = jnp.stack([transforms[:, 0], transforms[:, points - 1]], axis=1)
    wide_rows = [
        side_by_side(jnp.broadcast_to(ends[:, e, :, None], (slots, points, points)))
        for e in range(2)
    ]
    wide_cols = [side_by_side(ends[:, e]) for e in range(2)]
    lane = lax.broadcasted_iota(jnp.int32, (1, 1, slots * points), 2)
    result = 0.0
    for e in range(2):
        result = result + wide_rows[e][:, None, :] * side_by_side(hats[:, e, 0])[None, :, :]
        result = result + wide_rows[e][None, :, :] * side_by_side(hats[:, e, 1])[:, None, :]
        third = jnp.where(lane < points, hats[0, e, 2][:, :, None], hats[1, e, 2][:, :, None])
        result = result + wide_cols[e][None, None, :] * third
    solved = wide_inverse * result
    along_a = [jnp.sum(wide_rows[e][:, None, :] * solved, axis=0) for e in range(2)]
    along_b = [jnp.sum(wide_rows[e][None, :, :] * solved, axis=1) for e in range(2)]
    weighted = [wide_cols[e][None, None, :] * solved for e in range(2)]
    along_c = [
        [jnp.sum(weighted[e][:, :, :points], axis=2), jnp.sum(weighted[e][:, :, points:], axis=2)]
        for e in range(2)
    ]
    out = []
    for slot in range(slots):
        cut = slice(slot * points, (slot + 1) * points)
        out.append(
            jnp.stack(
                [
                    jnp.stack([along_a[e][:, cut], along_b[e][:, cut], along_c[e][slot]])
                    for e in range(2)
                ]
            )
        )
    planes_out = jnp.stack(out)
    traces = jnp.einsum(
        "sbj,sedjk,sck->sedbc", transforms, planes_out, transforms, precision=FAST
    )
    return traces.reshape(slots, 2, 3, points * points)


def slot_before(vector):
    return jnp.concatenate([jnp.zeros_like(vector[:1]), vector[:-1]], axis=0)


def slot_after(vector):
    return jnp.concatenate([vector[1:], jnp.zeros_like(vector[:1])], axis=0)


def on_device(load_vector, transform, diagonal, scaling, live_count, coarse_inverse):
    patch_loads = load_vector[0, 0]
    transforms = transform[0, 0]
    diagonals = diagonal[0, 0]
    weights = scaling[0, 0]
    coarse_rows = coarse_inverse[0, 0]
    slot_count = patch_loads.shape[0]
    coarse_size = coarse_rows.shape[-1]
    group_index = lax.axis_index("grp")
    owner_index = lax.axis_index("dev")
    groups = lax.axis_size("grp")
    owners = lax.axis_size("dev")
    prev_owner = (owner_index + owners - 1) % owners
    prev_group = (group_index + groups - 1) % groups

    rows = coarse_rows.reshape(slot_count, 3, coarse_size)
    extra_owner = jnp.concatenate([rows[:, 0], weights[:, 0:1]], axis=1)
    extra_group = jnp.concatenate([rows[:, 1], weights[:, 1:2]], axis=1)

    slot_index = jnp.arange(slot_count, dtype=jnp.int32)
    in_use = slot_index[None, None, :] < live_count[:, :, None]
    nothing = jnp.zeros_like(in_use[:, :, :1])
    alive = jnp.stack(
        [
            in_use & jnp.roll(in_use, -1, axis=1),
            in_use & jnp.roll(in_use, -1, axis=0),
            in_use & jnp.concatenate([in_use[:, :, 1:], nothing], axis=2),
        ],
        axis=-1,
    ).astype(jnp.float32)
    live_own = alive[group_index, owner_index]
    live_in = jnp.stack(
        [alive[group_index, prev_owner, :, 0], alive[prev_group, owner_index, :, 1]], axis=1
    )

    inverses = jax.vmap(inverse_diagonal)(diagonals)
    wide_inverse = side_by_side(inverses)

    def gather_all(payload):
        count = groups * owners
        spread = jnp.broadcast_to(payload[None], (count,) + payload.shape)
        got = lax.all_to_all(spread, ("grp", "dev"), 0, 0, tiled=True)
        return got.reshape(groups, owners, -1)

    def face_means(traces):
        return jnp.mean(traces, axis=-1).reshape(-1)

    def interface_means(raw):
        raw = raw.reshape(groups, owners, slot_count, 2, 3)
        low = raw[:, :, :, 0]
        high = raw[:, :, :, 1]
        following = jnp.stack(
            [
                jnp.roll(low[..., 0], -1, axis=1),
                jnp.roll(low[..., 1], -1, axis=0),
                jnp.concatenate([low[:, :, 1:, 2], jnp.zeros_like(low[:, :, :1, 2])], axis=2),
            ],
            axis=-1,
        )
        return (alive * (high - following)).reshape(groups, coarse_size)

    def coarse(means):
        here = means[group_index]
        before = means[prev_group]
        own = jnp.dot(coarse_rows, here, precision=PRECISE).reshape(slot_count, 3)
        first = jnp.dot(rows_in[:, 0], here, precision=PRECISE)
        second = jnp.dot(rows_in[:, 1], before, precision=PRECISE)
        return own, jnp.stack([first, second], axis=1)

    def jumps(traces_now, both, extra=None):
        low_side = traces_now[:, 0]
        high_side = traces_now[:, 1]
        face_size = high_side.shape[-1]
        sends = [low_side[:, 0], low_side[:, 1]]
        if both:
            sends += [
                jnp.concatenate([high_side[:, 0], extra[0]], axis=1),
                jnp.concatenate([high_side[:, 1], extra[1]], axis=1),
            ]
        sends = lax.optimization_barrier(sends)
        low_next_owner = shifted(sends[0], "dev", -1)
        low_next_group = shifted(sends[1], "grp", -1)
        following = jnp.stack(
            [low_next_owner, low_next_group, slot_after(low_side[:, 2])], axis=1
        )
        own = live_own[..., None] * (high_side - following)
        if not both:
            return own
        high_prev_owner = shifted(sends[2], "dev", 1)
        high_prev_group = shifted(sends[3], "grp", 1)
        leading = jnp.stack(
            [high_prev_owner[:, :face_size], high_prev_group[:, :face_size]], axis=1
        )
        incoming = live_in[..., None] * (leading - low_side[:, :2])
        return own, incoming, (high_prev_owner[:, face_size:], high_prev_group[:, face_size:])

    def solve(v_own, v_in):
        preceding = jnp.stack([v_in[:, 0], v_in[:, 1], slot_before(v_own[:, 2])], axis=1)
        return solve_pair(transforms, wide_inverse, -preceding, v_own)

    def split_terms(v_own, v_in, traces_now):
        low_side = traces_now[:, 0]
        high_side = traces_now[:, 1]
        second = jnp.concatenate(
            [
                live_in[..., None] * v_in * low_side[:, :2],
                (live_own[:, 2, None] * v_own[:, 2] * slot_after(low_side[:, 2]))[:, None],
            ],
            axis=1,
        )
        return live_own[..., None] * v_own * high_side - second

    def partial_sums(terms):
        return jnp.sum(jnp.stack(terms), axis=(1, 2, 3))

    def precondition(res_own, res_in, c_own, c_in):
        z_own = weights[..., None] * res_own + live_own[..., None] * c_own[..., None]
        z_in = weights_in[..., None] * res_in + live_in[..., None] * c_in[..., None]
        return z_own, z_in

    start_traces = jax.vmap(setup_one)(patch_loads, transforms, inverses)
    gathered = gather_all(face_means(start_traces))
    res_own, res_in, received = jumps(start_traces, True, (extra_owner, extra_group))
    rows_in = jnp.stack([received[0][:, :coarse_size], received[1][:, :coarse_size]], axis=1)
    weights_in = jnp.stack([received[0][:, coarse_size], received[1][:, coarse_size]], axis=1)
    c_own, c_in = coarse(interface_means(gathered))
    dir_own, dir_in = precondition(res_own, res_in, c_own, c_in)
    traces_one = solve(dir_own, dir_in)
    parts = partial_sums([res_own * dir_own, split_terms(dir_own, dir_in, traces_one)])
    gathered = gather_all(jnp.concatenate([face_means(traces_one), parts]))
    img_own, img_in, _ = jumps(traces_one, True, (extra_owner[:, :0], extra_group[:, :0]))
    totals = jnp.sum(gathered[:, :, slot_count * 6 :], axis=(0, 1))
    product = totals[0:1]
    curve = totals[1:2]
    step_len = (product / curve)[:, None, None]
    cq_own, cq_in = coarse(interface_means(gathered[:, :, : slot_count * 6]))
    multiplier = step_len * dir_own
    res_own = res_own - step_len * img_own
    res_in = res_in - step_len * img_in
    z_own, z_in = precondition(
        res_own, res_in, c_own - step_len[0] * cq_own, c_in - step_len[0] * cq_in
    )

    traces_two = solve(z_own, z_in)
    parts = partial_sums(
        [
            res_own * z_own,
            z_own * img_own,
            split_terms(z_own, z_in, traces_two),
            split_terms(dir_own, dir_in, traces_two),
        ]
    )
    gathered = gather_all(parts)
    fz_own = jumps(traces_two, False)
    totals = jnp.sum(gathered, axis=(0, 1))
    new_product = totals[0:1]
    ratio = new_product / product
    curve_two = totals[2:3] + ratio * (totals[1:2] + totals[3:4]) + ratio * ratio * curve
    step_two = (new_product / curve_two)[:, None, None]
    ratio = ratio[:, None, None]
    direction = z_own + ratio * dir_own
    applied = fz_own + ratio * img_own
    multiplier = multiplier + step_two * direction
    residual = res_own - step_two * applied
    return (multiplier[None, None], residual[None, None])


def solution(mesh):
    return jax.shard_map(
        on_device,
        mesh=mesh,
        in_specs=(
            P("grp", "dev", None, None, None),
            P("grp", "dev", None, None, None),
            P("grp", "dev", None, None),
            P("grp", "dev", None, None),
            P(),
            P("grp", "dev", None, None),
        ),
        out_specs=(P("grp", "dev", None, None, None), P("grp", "dev", None, None, None)),
        check_vma=False,
    )
```

```python
import jax
import jax.numpy as jnp
from jax import lax
from jax.sharding import PartitionSpec as P

PRECISE = lax.Precision.HIGHEST
FAST = lax.Precision.HIGH


def shifted(block, axis, distance):
    devices = range(lax.axis_size(axis))
    route = [((i - distance) % len(devices), i) for i in devices]
    return lax.ppermute(block, axis, route)


def inverse_diagonal(diagonal):
    return 1.0 / (diagonal[:, None, None] + diagonal[None, :, None] + diagonal[None, None, :])


def spectral(patch_load, transform):
    points = transform.shape[0]
    spatial = patch_load.astype(jnp.float32).reshape(points, points, points)
    moved = jnp.einsum("ai,abc->ibc", transform, spatial, precision=FAST)
    moved = jnp.einsum("bj,ibc->ijc", transform, moved, precision=FAST)
    return jnp.einsum("ck,ijc->ijk", transform, moved, precision=FAST)


def face_spectrum(transform, low_side, high_side):
    points = transform.shape[0]
    planes = jnp.stack([low_side, high_side]).reshape(2, 3, points, points)
    hats = jnp.einsum("bj,edbc,ck->edjk", transform, planes, transform, precision=FAST)
    low_row = transform[0]
    high_row = transform[points - 1]
    result = low_row[:, None, None] * hats[0, 0][None] + high_row[:, None, None] * hats[1, 0][None]
    result = (
        result
        + low_row[None, :, None] * hats[0, 1][:, None, :]
        + high_row[None, :, None] * hats[1, 1][:, None, :]
    )
    result = (
        result
        + low_row[None, None, :] * hats[0, 2][:, :, None]
        + high_row[None, None, :] * hats[1, 2][:, :, None]
    )
    return result


def trace_solved(transform, solved):
    points = transform.shape[0]
    end_rows = jnp.stack([transform[0], transform[points - 1]])
    along_a = jnp.sum(end_rows[:, :, None, None] * solved[None], axis=1)
    along_b = jnp.sum(end_rows[:, None, :, None] * solved[None], axis=2)
    along_c = jnp.sum(end_rows[:, None, None, :] * solved[None], axis=3)
    planes = jnp.stack([along_a, along_b, along_c], axis=1)
    traces = jnp.einsum("bj,edjk,ck->edbc", transform, planes, transform, precision=FAST)
    return traces.reshape(2, 3, points * points)


def setup_one(patch_load, one_transform, one_inverse):
    return trace_solved(one_transform, one_inverse * spectral(patch_load, one_transform))


def apply_one(one_transform, one_inverse, low_side, high_side):
    return trace_solved(
        one_transform, one_inverse * face_spectrum(one_transform, low_side, high_side)
    )


def slot_before(vector):
    return jnp.concatenate([jnp.zeros_like(vector[:1]), vector[:-1]], axis=0)


def slot_after(vector):
    return jnp.concatenate([vector[1:], jnp.zeros_like(vector[:1])], axis=0)


def on_device(load_vector, transform, diagonal, scaling, live_count, coarse_inverse):
    patch_loads = load_vector[0, 0]
    transforms = transform[0, 0]
    diagonals = diagonal[0, 0]
    weights = scaling[0, 0]
    coarse_rows = coarse_inverse[0, 0]
    slot_count = patch_loads.shape[0]
    coarse_size = coarse_rows.shape[-1]
    group_index = lax.axis_index("grp")
    owner_index = lax.axis_index("dev")
    groups = lax.axis_size("grp")
    owners = lax.axis_size("dev")
    prev_owner = (owner_index + owners - 1) % owners
    prev_group = (group_index + groups - 1) % groups

    rows = coarse_rows.reshape(slot_count, 3, coarse_size)
    extra_owner = jnp.concatenate([rows[:, 0], weights[:, 0:1]], axis=1)
    extra_group = jnp.concatenate([rows[:, 1], weights[:, 1:2]], axis=1)

    slot_index = jnp.arange(slot_count, dtype=jnp.int32)
    in_use = slot_index[None, None, :] < live_count[:, :, None]
    nothing = jnp.zeros_like(in_use[:, :, :1])
    alive = jnp.stack(
        [
            in_use & jnp.roll(in_use, -1, axis=1),
            in_use & jnp.roll(in_use, -1, axis=0),
            in_use & jnp.concatenate([in_use[:, :, 1:], nothing], axis=2),
        ],
        axis=-1,
    ).astype(jnp.float32)
    live_own = alive[group_index, owner_index]
    live_in = jnp.stack(
        [alive[group_index, prev_owner, :, 0], alive[prev_group, owner_index, :, 1]], axis=1
    )

    inverses = jax.vmap(inverse_diagonal)(diagonals)
    solver = jax.vmap(apply_one)

    def gather_all(payload):
        count = groups * owners
        spread = jnp.broadcast_to(payload[None], (count,) + payload.shape)
        got = lax.all_to_all(spread, ("grp", "dev"), 0, 0, tiled=True)
        return got.reshape(groups, owners, -1)

    def face_means(traces):
        return jnp.mean(traces, axis=-1).reshape(-1)

    def interface_means(raw):
        raw = raw.reshape(groups, owners, slot_count, 2, 3)
        low = raw[:, :, :, 0]
        high = raw[:, :, :, 1]
        following = jnp.stack(
            [
                jnp.roll(low[..., 0], -1, axis=1),
                jnp.roll(low[..., 1], -1, axis=0),
                jnp.concatenate([low[:, :, 1:, 2], jnp.zeros_like(low[:, :, :1, 2])], axis=2),
            ],
            axis=-1,
        )
        return (alive * (high - following)).reshape(groups, coarse_size)

    def coarse(means):
        here = means[group_index]
        before = means[prev_group]
        own = jnp.dot(coarse_rows, here, precision=PRECISE).reshape(slot_count, 3)
        first = jnp.dot(rows_in[:, 0], here, precision=PRECISE)
        second = jnp.dot(rows_in[:, 1], before, precision=PRECISE)
        return own, jnp.stack([first, second], axis=1)

    def jumps(traces_now, both, extra=None, after=None):
        low_side = traces_now[:, 0]
        high_side = traces_now[:, 1]
        face_size = high_side.shape[-1]
        sends = [low_side[:, 0], low_side[:, 1]]
        if both:
            sends += [
                jnp.concatenate([high_side[:, 0], extra[0]], axis=1),
                jnp.concatenate([high_side[:, 1], extra[1]], axis=1),
            ]
        sends, after = lax.optimization_barrier((sends, after))
        low_next_owner = shifted(sends[0], "dev", -1)
        low_next_group = shifted(sends[1], "grp", -1)
        following = jnp.stack(
            [low_next_owner, low_next_group, slot_after(low_side[:, 2])], axis=1
        )
        own = live_own[..., None] * (high_side - following)
        if not both:
            return own
        high_prev_owner = shifted(sends[2], "dev", 1)
        high_prev_group = shifted(sends[3], "grp", 1)
        leading = jnp.stack(
            [high_prev_owner[:, :face_size], high_prev_group[:, :face_size]], axis=1
        )
        incoming = live_in[..., None] * (leading - low_side[:, :2])
        tail = (high_prev_owner[:, face_size:], high_prev_group[:, face_size:])
        return own, incoming, tail, after

    def solve(v_own, v_in):
        preceding = jnp.stack([v_in[:, 0], v_in[:, 1], slot_before(v_own[:, 2])], axis=1)
        return solver(transforms, inverses, -preceding, v_own)

    def split_terms(v_own, v_in, traces_now):
        low_side = traces_now[:, 0]
        high_side = traces_now[:, 1]
        second = jnp.concatenate(
            [
                live_in[..., None] * v_in * low_side[:, :2],
                (live_own[:, 2, None] * v_own[:, 2] * slot_after(low_side[:, 2]))[:, None],
            ],
            axis=1,
        )
        return live_own[..., None] * v_own * high_side - second

    def partial_sums(terms):
        return jnp.sum(jnp.stack(terms), axis=(1, 2, 3))

    def precondition(res_own, res_in, c_own, c_in):
        z_own = weights[..., None] * res_own + live_own[..., None] * c_own[..., None]
        z_in = weights_in[..., None] * res_in + live_in[..., None] * c_in[..., None]
        return z_own, z_in

    start_traces = jax.vmap(setup_one)(patch_loads, transforms, inverses)
    gathered = gather_all(face_means(start_traces))
    res_own, res_in, received, gathered = jumps(
        start_traces, True, (extra_owner, extra_group), gathered
    )
    rows_in = jnp.stack([received[0][:, :coarse_size], received[1][:, :coarse_size]], axis=1)
    weights_in = jnp.stack([received[0][:, coarse_size], received[1][:, coarse_size]], axis=1)
    c_own, c_in = coarse(interface_means(gathered))
    dir_own, dir_in = precondition(res_own, res_in, c_own, c_in)
    traces_one = solve(dir_own, dir_in)
    parts = partial_sums([res_own * dir_own, split_terms(dir_own, dir_in, traces_one)])
    gathered = gather_all(jnp.concatenate([face_means(traces_one), parts]))
    img_own, img_in, _, _ = jumps(traces_one, True, (extra_owner[:, :0], extra_group[:, :0]))
    totals = jnp.sum(gathered[:, :, slot_count * 6 :], axis=(0, 1))
    product = totals[0:1]
    curve = totals[1:2]
    step_len = (product / curve)[:, None, None]
    cq_own, cq_in = coarse(interface_means(gathered[:, :, : slot_count * 6]))
    multiplier = step_len * dir_own
    res_own = res_own - step_len * img_own
    res_in = res_in - step_len * img_in
    z_own, z_in = precondition(
        res_own, res_in, c_own - step_len[0] * cq_own, c_in - step_len[0] * cq_in
    )

    traces_two = solve(z_own, z_in)
    parts = partial_sums(
        [
            res_own * z_own,
            z_own * img_own,
            split_terms(z_own, z_in, traces_two),
            split_terms(dir_own, dir_in, traces_two),
        ]
    )
    gathered = gather_all(parts)
    fz_own = jumps(traces_two, False)
    totals = jnp.sum(gathered, axis=(0, 1))
    new_product = totals[0:1]
    ratio = new_product / product
    curve_two = totals[2:3] + ratio * (totals[1:2] + totals[3:4]) + ratio * ratio * curve
    step_two = (new_product / curve_two)[:, None, None]
    ratio = ratio[:, None, None]
    direction = z_own + ratio * dir_own
    applied = fz_own + ratio * img_own
    multiplier = multiplier + step_two * direction
    residual = res_own - step_two * applied
    return (multiplier[None, None], residual[None, None])


def solution(mesh):
    return jax.shard_map(
        on_device,
        mesh=mesh,
        in_specs=(
            P("grp", "dev", None, None, None),
            P("grp", "dev", None, None, None),
            P("grp", "dev", None, None),
            P("grp", "dev", None, None),
            P(),
            P("grp", "dev", None, None),
        ),
        out_specs=(P("grp", "dev", None, None, None), P("grp", "dev", None, None, None)),
        check_vma=False,
    )
```

```python
import jax
import jax.numpy as jnp
from jax import lax
from jax.sharding import PartitionSpec as P

PRECISE = lax.Precision.HIGHEST
FAST = lax.Precision.HIGH


def shifted(block, axis, distance):
    devices = range(lax.axis_size(axis))
    route = [((i - distance) % len(devices), i) for i in devices]
    return lax.ppermute(block, axis, route)


def inverse_diagonal(diagonal):
    return 1.0 / (diagonal[:, None, None] + diagonal[None, :, None] + diagonal[None, None, :])


def spectral(patch_load, transform):
    points = transform.shape[0]
    spatial = patch_load.astype(jnp.float32).reshape(points, points, points)
    moved = jnp.einsum("ai,abc->ibc", transform, spatial, precision=FAST)
    moved = jnp.einsum("bj,ibc->ijc", transform, moved, precision=FAST)
    return jnp.einsum("ck,ijc->ijk", transform, moved, precision=FAST)


def face_spectrum(transform, low_side, high_side):
    points = transform.shape[0]
    planes = jnp.stack([low_side, high_side]).reshape(2, 3, points, points)
    hats = jnp.einsum("bj,edbc,ck->edjk", transform, planes, transform, precision=FAST)
    low_row = transform[0]
    high_row = transform[points - 1]
    result = low_row[:, None, None] * hats[0, 0][None] + high_row[:, None, None] * hats[1, 0][None]
    result = (
        result
        + low_row[None, :, None] * hats[0, 1][:, None, :]
        + high_row[None, :, None] * hats[1, 1][:, None, :]
    )
    result = (
        result
        + low_row[None, None, :] * hats[0, 2][:, :, None]
        + high_row[None, None, :] * hats[1, 2][:, :, None]
    )
    return result


def trace_solved(transform, solved):
    points = transform.shape[0]
    end_rows = jnp.stack([transform[0], transform[points - 1]])
    along_a = jnp.sum(end_rows[:, :, None, None] * solved[None], axis=1)
    along_b = jnp.sum(end_rows[:, None, :, None] * solved[None], axis=2)
    along_c = jnp.sum(end_rows[:, None, None, :] * solved[None], axis=3)
    planes = jnp.stack([along_a, along_b, along_c], axis=1)
    traces = jnp.einsum("bj,edjk,ck->edbc", transform, planes, transform, precision=FAST)
    return traces.reshape(2, 3, points * points)


def setup_one(patch_load, one_transform, one_inverse):
    return trace_solved(one_transform, one_inverse * spectral(patch_load, one_transform))


def apply_one(one_transform, one_inverse, low_side, high_side):
    return trace_solved(
        one_transform, one_inverse * face_spectrum(one_transform, low_side, high_side)
    )


def slot_before(vector):
    return jnp.concatenate([jnp.zeros_like(vector[:1]), vector[:-1]], axis=0)


def slot_after(vector):
    return jnp.concatenate([vector[1:], jnp.zeros_like(vector[:1])], axis=0)


def on_device(load_vector, transform, diagonal, scaling, live_count, coarse_inverse):
    patch_loads = load_vector[0, 0]
    transforms = transform[0, 0]
    diagonals = diagonal[0, 0]
    weights = scaling[0, 0]
    coarse_rows = coarse_inverse[0, 0]
    slot_count = patch_loads.shape[0]
    coarse_size = coarse_rows.shape[-1]
    group_index = lax.axis_index("grp")
    owner_index = lax.axis_index("dev")
    groups = lax.axis_size("grp")
    owners = lax.axis_size("dev")
    prev_owner = (owner_index + owners - 1) % owners
    prev_group = (group_index + groups - 1) % groups

    rows = coarse_rows.reshape(slot_count, 3, coarse_size)
    extra_owner = jnp.concatenate([rows[:, 0], weights[:, 0:1]], axis=1)
    extra_group = jnp.concatenate([rows[:, 1], weights[:, 1:2]], axis=1)

    slot_index = jnp.arange(slot_count, dtype=jnp.int32)
    in_use = slot_index[None, None, :] < live_count[:, :, None]
    nothing = jnp.zeros_like(in_use[:, :, :1])
    alive = jnp.stack(
        [
            in_use & jnp.roll(in_use, -1, axis=1),
            in_use & jnp.roll(in_use, -1, axis=0),
            in_use & jnp.concatenate([in_use[:, :, 1:], nothing], axis=2),
        ],
        axis=-1,
    ).astype(jnp.float32)
    live_own = alive[group_index, owner_index]
    live_in = jnp.stack(
        [alive[group_index, prev_owner, :, 0], alive[prev_group, owner_index, :, 1]], axis=1
    )

    inverses = jax.vmap(inverse_diagonal)(diagonals)
    solver = jax.vmap(apply_one)

    def gather_all(payload):
        count = groups * owners
        spread = jnp.broadcast_to(payload[None], (count,) + payload.shape)
        got = lax.all_to_all(spread, ("grp", "dev"), 0, 0, tiled=True)
        return got.reshape(groups, owners, -1)

    def face_means(traces):
        return jnp.mean(traces, axis=-1).reshape(-1)

    def interface_means(raw):
        raw = raw.reshape(groups, owners, slot_count, 2, 3)
        low = raw[:, :, :, 0]
        high = raw[:, :, :, 1]
        following = jnp.stack(
            [
                jnp.roll(low[..., 0], -1, axis=1),
                jnp.roll(low[..., 1], -1, axis=0),
                jnp.concatenate([low[:, :, 1:, 2], jnp.zeros_like(low[:, :, :1, 2])], axis=2),
            ],
            axis=-1,
        )
        return (alive * (high - following)).reshape(groups, coarse_size)

    def coarse(means):
        here = means[group_index]
        before = means[prev_group]
        own = jnp.dot(coarse_rows, here, precision=PRECISE).reshape(slot_count, 3)
        first = jnp.dot(rows_in[:, 0], here, precision=PRECISE)
        second = jnp.dot(rows_in[:, 1], before, precision=PRECISE)
        return own, jnp.stack([first, second], axis=1)

    def jumps(traces_now, both, extra=None, after=None):
        low_side = traces_now[:, 0]
        high_side = traces_now[:, 1]
        face_size = high_side.shape[-1]
        sends = [low_side[:, 0], low_side[:, 1]]
        if both:
            sends += [
                jnp.concatenate([high_side[:, 0], extra[0]], axis=1),
                jnp.concatenate([high_side[:, 1], extra[1]], axis=1),
            ]
        sends, after = lax.optimization_barrier((sends, after))
        low_next_owner = shifted(sends[0], "dev", -1)
        low_next_group = shifted(sends[1], "grp", -1)
        following = jnp.stack(
            [low_next_owner, low_next_group, slot_after(low_side[:, 2])], axis=1
        )
        own = live_own[..., None] * (high_side - following)
        if not both:
            return own, after
        high_prev_owner = shifted(sends[2], "dev", 1)
        high_prev_group = shifted(sends[3], "grp", 1)
        leading = jnp.stack(
            [high_prev_owner[:, :face_size], high_prev_group[:, :face_size]], axis=1
        )
        incoming = live_in[..., None] * (leading - low_side[:, :2])
        tail = (high_prev_owner[:, face_size:], high_prev_group[:, face_size:])
        return own, incoming, tail, after

    def solve(v_own, v_in):
        preceding = jnp.stack([v_in[:, 0], v_in[:, 1], slot_before(v_own[:, 2])], axis=1)
        return solver(transforms, inverses, -preceding, v_own)

    def split_terms(v_own, v_in, traces_now):
        low_side = traces_now[:, 0]
        high_side = traces_now[:, 1]
        second = jnp.concatenate(
            [
                live_in[..., None] * v_in * low_side[:, :2],
                (live_own[:, 2, None] * v_own[:, 2] * slot_after(low_side[:, 2]))[:, None],
            ],
            axis=1,
        )
        return live_own[..., None] * v_own * high_side - second

    def partial_sums(terms):
        return jnp.sum(jnp.stack(terms), axis=(1, 2, 3))

    def precondition(res_own, res_in, c_own, c_in):
        z_own = weights[..., None] * res_own + live_own[..., None] * c_own[..., None]
        z_in = weights_in[..., None] * res_in + live_in[..., None] * c_in[..., None]
        return z_own, z_in

    start_traces = jax.vmap(setup_one)(patch_loads, transforms, inverses)
    gathered = gather_all(face_means(start_traces))
    res_own, res_in, received, gathered = jumps(
        start_traces, True, (extra_owner, extra_group), gathered
    )
    rows_in = jnp.stack([received[0][:, :coarse_size], received[1][:, :coarse_size]], axis=1)
    weights_in = jnp.stack([received[0][:, coarse_size], received[1][:, coarse_size]], axis=1)
    c_own, c_in = coarse(interface_means(gathered))
    dir_own, dir_in = precondition(res_own, res_in, c_own, c_in)
    traces_one = solve(dir_own, dir_in)
    parts = partial_sums([res_own * dir_own, split_terms(dir_own, dir_in, traces_one)])
    gathered = gather_all(jnp.concatenate([face_means(traces_one), parts]))
    img_own, img_in, _, gathered = jumps(
        traces_one, True, (extra_owner[:, :0], extra_group[:, :0]), gathered
    )
    totals = jnp.sum(gathered[:, :, slot_count * 6 :], axis=(0, 1))
    product = totals[0:1]
    curve = totals[1:2]
    step_len = (product / curve)[:, None, None]
    cq_own, cq_in = coarse(interface_means(gathered[:, :, : slot_count * 6]))
    multiplier = step_len * dir_own
    res_own = res_own - step_len * img_own
    res_in = res_in - step_len * img_in
    z_own, z_in = precondition(
        res_own, res_in, c_own - step_len[0] * cq_own, c_in - step_len[0] * cq_in
    )

    traces_two = solve(z_own, z_in)
    parts = partial_sums(
        [
            res_own * z_own,
            z_own * img_own,
            split_terms(z_own, z_in, traces_two),
            split_terms(dir_own, dir_in, traces_two),
        ]
    )
    gathered = gather_all(parts)
    fz_own, gathered = jumps(traces_two, False, None, gathered)
    totals = jnp.sum(gathered, axis=(0, 1))
    new_product = totals[0:1]
    ratio = new_product / product
    curve_two = totals[2:3] + ratio * (totals[1:2] + totals[3:4]) + ratio * ratio * curve
    step_two = (new_product / curve_two)[:, None, None]
    ratio = ratio[:, None, None]
    direction = z_own + ratio * dir_own
    applied = fz_own + ratio * img_own
    multiplier = multiplier + step_two * direction
    residual = res_own - step_two * applied
    return (multiplier[None, None], residual[None, None])


def solution(mesh):
    return jax.shard_map(
        on_device,
        mesh=mesh,
        in_specs=(
            P("grp", "dev", None, None, None),
            P("grp", "dev", None, None, None),
            P("grp", "dev", None, None),
            P("grp", "dev", None, None),
            P(),
            P("grp", "dev", None, None),
        ),
        out_specs=(P("grp", "dev", None, None, None), P("grp", "dev", None, None, None)),
        check_vma=False,
    )
```

```python
import jax
import jax.numpy as jnp
from jax import lax
from jax.sharding import PartitionSpec as P

PRECISE = lax.Precision.HIGHEST
FAST = lax.Precision.HIGH


def shifted(block, axis, distance):
    devices = range(lax.axis_size(axis))
    route = [((i - distance) % len(devices), i) for i in devices]
    return lax.ppermute(block, axis, route)


def inverse_diagonal(diagonal):
    return 1.0 / (diagonal[:, None, None] + diagonal[None, :, None] + diagonal[None, None, :])


def spectral(patch_load, transform):
    points = transform.shape[0]
    spatial = patch_load.astype(jnp.float32).reshape(points, points, points)
    moved = jnp.einsum("ai,abc->ibc", transform, spatial, precision=FAST)
    moved = jnp.einsum("bj,ibc->ijc", transform, moved, precision=FAST)
    return jnp.einsum("ck,ijc->ijk", transform, moved, precision=FAST)


def face_spectrum(transform, low_side, high_side):
    points = transform.shape[0]
    planes = jnp.stack([low_side, high_side]).reshape(2, 3, points, points)
    hats = jnp.einsum("bj,edbc,ck->edjk", transform, planes, transform, precision=FAST)
    low_row = transform[0]
    high_row = transform[points - 1]
    result = low_row[:, None, None] * hats[0, 0][None] + high_row[:, None, None] * hats[1, 0][None]
    result = (
        result
        + low_row[None, :, None] * hats[0, 1][:, None, :]
        + high_row[None, :, None] * hats[1, 1][:, None, :]
    )
    result = (
        result
        + low_row[None, None, :] * hats[0, 2][:, :, None]
        + high_row[None, None, :] * hats[1, 2][:, :, None]
    )
    return result


def trace_solved(transform, solved):
    points = transform.shape[0]
    end_rows = jnp.stack([transform[0], transform[points - 1]])
    along_a = jnp.sum(end_rows[:, :, None, None] * solved[None], axis=1)
    along_b = jnp.sum(end_rows[:, None, :, None] * solved[None], axis=2)
    along_c = jnp.sum(end_rows[:, None, None, :] * solved[None], axis=3)
    planes = jnp.stack([along_a, along_b, along_c], axis=1)
    traces = jnp.einsum("bj,edjk,ck->edbc", transform, planes, transform, precision=FAST)
    return traces.reshape(2, 3, points * points)


def plane_means(transform, solved):
    points = transform.shape[0]
    end_rows = jnp.stack([transform[0], transform[points - 1]])
    spread = jnp.mean(transform, axis=0)
    along_a = jnp.sum(end_rows[:, :, None, None] * solved[None], axis=1)
    along_b = jnp.sum(end_rows[:, None, :, None] * solved[None], axis=2)
    along_c = jnp.sum(end_rows[:, None, None, :] * solved[None], axis=3)
    planes = jnp.stack([along_a, along_b, along_c], axis=1)
    return jnp.sum(planes * spread[:, None] * spread[None, :], axis=(2, 3))


def setup_one(patch_load, one_transform, one_inverse):
    solved = one_inverse * spectral(patch_load, one_transform)
    return trace_solved(one_transform, solved), plane_means(one_transform, solved)


def apply_one(one_transform, one_inverse, low_side, high_side):
    return trace_solved(
        one_transform, one_inverse * face_spectrum(one_transform, low_side, high_side)
    )


def slot_before(vector):
    return jnp.concatenate([jnp.zeros_like(vector[:1]), vector[:-1]], axis=0)


def slot_after(vector):
    return jnp.concatenate([vector[1:], jnp.zeros_like(vector[:1])], axis=0)


def on_device(load_vector, transform, diagonal, scaling, live_count, coarse_inverse):
    patch_loads = load_vector[0, 0]
    transforms = transform[0, 0]
    diagonals = diagonal[0, 0]
    weights = scaling[0, 0]
    coarse_rows = coarse_inverse[0, 0]
    slot_count = patch_loads.shape[0]
    coarse_size = coarse_rows.shape[-1]
    group_index = lax.axis_index("grp")
    owner_index = lax.axis_index("dev")
    groups = lax.axis_size("grp")
    owners = lax.axis_size("dev")
    prev_owner = (owner_index + owners - 1) % owners
    prev_group = (group_index + groups - 1) % groups

    rows = coarse_rows.reshape(slot_count, 3, coarse_size)
    extra_owner = jnp.concatenate([rows[:, 0], weights[:, 0:1]], axis=1)
    extra_group = jnp.concatenate([rows[:, 1], weights[:, 1:2]], axis=1)

    slot_index = jnp.arange(slot_count, dtype=jnp.int32)
    in_use = slot_index[None, None, :] < live_count[:, :, None]
    nothing = jnp.zeros_like(in_use[:, :, :1])
    alive = jnp.stack(
        [
            in_use & jnp.roll(in_use, -1, axis=1),
            in_use & jnp.roll(in_use, -1, axis=0),
            in_use & jnp.concatenate([in_use[:, :, 1:], nothing], axis=2),
        ],
        axis=-1,
    ).astype(jnp.float32)
    live_own = alive[group_index, owner_index]
    live_in = jnp.stack(
        [alive[group_index, prev_owner, :, 0], alive[prev_group, owner_index, :, 1]], axis=1
    )

    inverses = jax.vmap(inverse_diagonal)(diagonals)
    solver = jax.vmap(apply_one)

    def gather_all(payload):
        count = groups * owners
        spread = jnp.broadcast_to(payload[None], (count,) + payload.shape)
        got = lax.all_to_all(spread, ("grp", "dev"), 0, 0, tiled=True)
        return got.reshape(groups, owners, -1)

    def face_means(traces):
        return jnp.mean(traces, axis=-1).reshape(-1)

    def interface_means(raw):
        raw = raw.reshape(groups, owners, slot_count, 2, 3)
        low = raw[:, :, :, 0]
        high = raw[:, :, :, 1]
        following = jnp.stack(
            [
                jnp.roll(low[..., 0], -1, axis=1),
                jnp.roll(low[..., 1], -1, axis=0),
                jnp.concatenate([low[:, :, 1:, 2], jnp.zeros_like(low[:, :, :1, 2])], axis=2),
            ],
            axis=-1,
        )
        return (alive * (high - following)).reshape(groups, coarse_size)

    def coarse(means):
        here = means[group_index]
        before = means[prev_group]
        own = jnp.dot(coarse_rows, here, precision=PRECISE).reshape(slot_count, 3)
        first = jnp.dot(rows_in[:, 0], here, precision=PRECISE)
        second = jnp.dot(rows_in[:, 1], before, precision=PRECISE)
        return own, jnp.stack([first, second], axis=1)

    def jumps(traces_now, both, extra=None, after=None):
        low_side = traces_now[:, 0]
        high_side = traces_now[:, 1]
        face_size = high_side.shape[-1]
        sends = [low_side[:, 0], low_side[:, 1]]
        if both:
            sends += [
                jnp.concatenate([high_side[:, 0], extra[0]], axis=1),
                jnp.concatenate([high_side[:, 1], extra[1]], axis=1),
            ]
        sends, after = lax.optimization_barrier((sends, after))
        low_next_owner = shifted(sends[0], "dev", -1)
        low_next_group = shifted(sends[1], "grp", -1)
        following = jnp.stack(
            [low_next_owner, low_next_group, slot_after(low_side[:, 2])], axis=1
        )
        own = live_own[..., None] * (high_side - following)
        if not both:
            return own
        high_prev_owner = shifted(sends[2], "dev", 1)
        high_prev_group = shifted(sends[3], "grp", 1)
        leading = jnp.stack(
            [high_prev_owner[:, :face_size], high_prev_group[:, :face_size]], axis=1
        )
        incoming = live_in[..., None] * (leading - low_side[:, :2])
        tail = (high_prev_owner[:, face_size:], high_prev_group[:, face_size:])
        return own, incoming, tail, after

    def solve(v_own, v_in):
        preceding = jnp.stack([v_in[:, 0], v_in[:, 1], slot_before(v_own[:, 2])], axis=1)
        return solver(transforms, inverses, -preceding, v_own)

    def split_terms(v_own, v_in, traces_now):
        low_side = traces_now[:, 0]
        high_side = traces_now[:, 1]
        second = jnp.concatenate(
            [
                live_in[..., None] * v_in * low_side[:, :2],
                (live_own[:, 2, None] * v_own[:, 2] * slot_after(low_side[:, 2]))[:, None],
            ],
            axis=1,
        )
        return live_own[..., None] * v_own * high_side - second

    def partial_sums(terms):
        return jnp.sum(jnp.stack(terms), axis=(1, 2, 3))

    def precondition(res_own, res_in, c_own, c_in):
        z_own = weights[..., None] * res_own + live_own[..., None] * c_own[..., None]
        z_in = weights_in[..., None] * res_in + live_in[..., None] * c_in[..., None]
        return z_own, z_in

    start_traces, start_means = jax.vmap(setup_one)(patch_loads, transforms, inverses)
    gathered = gather_all(start_means.reshape(-1))
    res_own, res_in, received, gathered = jumps(
        start_traces, True, (extra_owner, extra_group), gathered
    )
    rows_in = jnp.stack([received[0][:, :coarse_size], received[1][:, :coarse_size]], axis=1)
    weights_in = jnp.stack([received[0][:, coarse_size], received[1][:, coarse_size]], axis=1)
    c_own, c_in = coarse(interface_means(gathered))
    dir_own, dir_in = precondition(res_own, res_in, c_own, c_in)
    traces_one = solve(dir_own, dir_in)
    parts = partial_sums([res_own * dir_own, split_terms(dir_own, dir_in, traces_one)])
    gathered = gather_all(jnp.concatenate([face_means(traces_one), parts]))
    img_own, img_in, _, _ = jumps(traces_one, True, (extra_owner[:, :0], extra_group[:, :0]))
    totals = jnp.sum(gathered[:, :, slot_count * 6 :], axis=(0, 1))
    product = totals[0:1]
    curve = totals[1:2]
    step_len = (product / curve)[:, None, None]
    cq_own, cq_in = coarse(interface_means(gathered[:, :, : slot_count * 6]))
    multiplier = step_len * dir_own
    res_own = res_own - step_len * img_own
    res_in = res_in - step_len * img_in
    z_own, z_in = precondition(
        res_own, res_in, c_own - step_len[0] * cq_own, c_in - step_len[0] * cq_in
    )

    traces_two = solve(z_own, z_in)
    parts = partial_sums(
        [
            res_own * z_own,
            z_own * img_own,
            split_terms(z_own, z_in, traces_two),
            split_terms(dir_own, dir_in, traces_two),
        ]
    )
    gathered = gather_all(parts)
    fz_own = jumps(traces_two, False)
    totals = jnp.sum(gathered, axis=(0, 1))
    new_product = totals[0:1]
    ratio = new_product / product
    curve_two = totals[2:3] + ratio * (totals[1:2] + totals[3:4]) + ratio * ratio * curve
    step_two = (new_product / curve_two)[:, None, None]
    ratio = ratio[:, None, None]
    direction = z_own + ratio * dir_own
    applied = fz_own + ratio * img_own
    multiplier = multiplier + step_two * direction
    residual = res_own - step_two * applied
    return (multiplier[None, None], residual[None, None])


def solution(mesh):
    return jax.shard_map(
        on_device,
        mesh=mesh,
        in_specs=(
            P("grp", "dev", None, None, None),
            P("grp", "dev", None, None, None),
            P("grp", "dev", None, None),
            P("grp", "dev", None, None),
            P(),
            P("grp", "dev", None, None),
        ),
        out_specs=(P("grp", "dev", None, None, None), P("grp", "dev", None, None, None)),
        check_vma=False,
    )
```

```python
import jax
import jax.numpy as jnp
from jax import lax
from jax.sharding import PartitionSpec as P

PRECISE = lax.Precision.HIGHEST
FAST = lax.Precision.HIGH


def shifted(block, axis, distance):
    devices = range(lax.axis_size(axis))
    route = [((i - distance) % len(devices), i) for i in devices]
    return lax.ppermute(block, axis, route)


def inverse_diagonal(diagonal):
    return 1.0 / (diagonal[:, None, None] + diagonal[None, :, None] + diagonal[None, None, :])


def spectral(patch_load, transform):
    points = transform.shape[0]
    spatial = patch_load.astype(jnp.float32).reshape(points, points, points)
    moved = jnp.einsum("ai,abc->ibc", transform, spatial, precision=FAST)
    moved = jnp.einsum("bj,ibc->ijc", transform, moved, precision=FAST)
    return jnp.einsum("ck,ijc->ijk", transform, moved, precision=FAST)


def face_spectrum(transform, low_side, high_side):
    points = transform.shape[0]
    planes = jnp.stack([low_side, high_side]).reshape(2, 3, points, points)
    hats = jnp.einsum("bj,edbc,ck->edjk", transform, planes, transform, precision=FAST)
    low_row = transform[0]
    high_row = transform[points - 1]
    result = low_row[:, None, None] * hats[0, 0][None] + high_row[:, None, None] * hats[1, 0][None]
    result = (
        result
        + low_row[None, :, None] * hats[0, 1][:, None, :]
        + high_row[None, :, None] * hats[1, 1][:, None, :]
    )
    result = (
        result
        + low_row[None, None, :] * hats[0, 2][:, :, None]
        + high_row[None, None, :] * hats[1, 2][:, :, None]
    )
    return result


def trace_solved(transform, solved):
    points = transform.shape[0]
    end_rows = jnp.stack([transform[0], transform[points - 1]])
    along_a = jnp.sum(end_rows[:, :, None, None] * solved[None], axis=1)
    along_b = jnp.sum(end_rows[:, None, :, None] * solved[None], axis=2)
    along_c = jnp.sum(end_rows[:, None, None, :] * solved[None], axis=3)
    planes = jnp.stack([along_a, along_b, along_c], axis=1)
    traces = jnp.einsum("bj,edjk,ck->edbc", transform, planes, transform, precision=FAST)
    return traces.reshape(2, 3, points * points)


def plane_means(transform, solved):
    points = transform.shape[0]
    end_rows = jnp.stack([transform[0], transform[points - 1]])
    spread = jnp.mean(transform, axis=0)
    along_a = jnp.sum(end_rows[:, :, None, None] * solved[None], axis=1)
    along_b = jnp.sum(end_rows[:, None, :, None] * solved[None], axis=2)
    along_c = jnp.sum(end_rows[:, None, None, :] * solved[None], axis=3)
    planes = jnp.stack([along_a, along_b, along_c], axis=1)
    return jnp.sum(planes * spread[:, None] * spread[None, :], axis=(2, 3))


def setup_one(patch_load, one_transform, one_inverse):
    solved = one_inverse * spectral(patch_load, one_transform)
    return trace_solved(one_transform, solved), plane_means(one_transform, solved)


def apply_one(one_transform, one_inverse, low_side, high_side):
    return trace_solved(
        one_transform, one_inverse * face_spectrum(one_transform, low_side, high_side)
    )


def slot_before(vector):
    return jnp.concatenate([jnp.zeros_like(vector[:1]), vector[:-1]], axis=0)


def slot_after(vector):
    return jnp.concatenate([vector[1:], jnp.zeros_like(vector[:1])], axis=0)


def on_device(load_vector, transform, diagonal, scaling, live_count, coarse_inverse):
    patch_loads = load_vector[0, 0]
    transforms = transform[0, 0]
    diagonals = diagonal[0, 0]
    weights = scaling[0, 0]
    coarse_rows = coarse_inverse[0, 0]
    slot_count = patch_loads.shape[0]
    coarse_size = coarse_rows.shape[-1]
    group_index = lax.axis_index("grp")
    owner_index = lax.axis_index("dev")
    groups = lax.axis_size("grp")
    owners = lax.axis_size("dev")
    prev_owner = (owner_index + owners - 1) % owners
    prev_group = (group_index + groups - 1) % groups

    rows = coarse_rows.reshape(slot_count, 3, coarse_size)
    extra_owner = jnp.concatenate([rows[:, 0], weights[:, 0:1]], axis=1)
    extra_group = jnp.concatenate([rows[:, 1], weights[:, 1:2]], axis=1)

    slot_index = jnp.arange(slot_count, dtype=jnp.int32)
    in_use = slot_index[None, None, :] < live_count[:, :, None]
    nothing = jnp.zeros_like(in_use[:, :, :1])
    alive = jnp.stack(
        [
            in_use & jnp.roll(in_use, -1, axis=1),
            in_use & jnp.roll(in_use, -1, axis=0),
            in_use & jnp.concatenate([in_use[:, :, 1:], nothing], axis=2),
        ],
        axis=-1,
    ).astype(jnp.float32)
    live_own = alive[group_index, owner_index]
    live_in = jnp.stack(
        [alive[group_index, prev_owner, :, 0], alive[prev_group, owner_index, :, 1]], axis=1
    )

    inverses = jax.vmap(inverse_diagonal)(diagonals)
    solver = jax.vmap(apply_one)

    def gather_all(payload):
        count = groups * owners
        spread = jnp.broadcast_to(payload[None], (count,) + payload.shape)
        got = lax.all_to_all(spread, ("grp", "dev"), 0, 0, tiled=True)
        return got.reshape(groups, owners, -1)

    def face_means(traces):
        return jnp.mean(traces, axis=-1).reshape(-1)

    def interface_means(raw):
        raw = raw.reshape(groups, owners, slot_count, 2, 3)
        low = raw[:, :, :, 0]
        high = raw[:, :, :, 1]
        following = jnp.stack(
            [
                jnp.roll(low[..., 0], -1, axis=1),
                jnp.roll(low[..., 1], -1, axis=0),
                jnp.concatenate([low[:, :, 1:, 2], jnp.zeros_like(low[:, :, :1, 2])], axis=2),
            ],
            axis=-1,
        )
        return (alive * (high - following)).reshape(groups, coarse_size)

    def coarse(means):
        here = means[group_index]
        before = means[prev_group]
        own = jnp.dot(coarse_rows, here, precision=PRECISE).reshape(slot_count, 3)
        first = jnp.dot(rows_in[:, 0], here, precision=PRECISE)
        second = jnp.dot(rows_in[:, 1], before, precision=PRECISE)
        return own, jnp.stack([first, second], axis=1)

    def jumps(traces_now, both, extra=None, after=None):
        low_side = traces_now[:, 0]
        high_side = traces_now[:, 1]
        face_size = high_side.shape[-1]
        sends = [low_side[:, 0], low_side[:, 1]]
        if both:
            sends += [
                jnp.concatenate([high_side[:, 0], extra[0]], axis=1),
                jnp.concatenate([high_side[:, 1], extra[1]], axis=1),
            ]
        sends, after = lax.optimization_barrier((sends, after))
        low_next_owner = shifted(sends[0], "dev", -1)
        low_next_group = shifted(sends[1], "grp", -1)
        following = jnp.stack(
            [low_next_owner, low_next_group, slot_after(low_side[:, 2])], axis=1
        )
        own = live_own[..., None] * (high_side - following)
        if not both:
            return own
        high_prev_owner = shifted(sends[2], "dev", 1)
        high_prev_group = shifted(sends[3], "grp", 1)
        leading = jnp.stack(
            [high_prev_owner[:, :face_size], high_prev_group[:, :face_size]], axis=1
        )
        incoming = live_in[..., None] * (leading - low_side[:, :2])
        tail = (high_prev_owner[:, face_size:], high_prev_group[:, face_size:])
        return own, incoming, tail, after

    def solve(v_own, v_in):
        preceding = jnp.stack([v_in[:, 0], v_in[:, 1], slot_before(v_own[:, 2])], axis=1)
        return solver(transforms, inverses, -preceding, v_own)

    def split_terms(v_own, v_in, traces_now):
        low_side = traces_now[:, 0]
        high_side = traces_now[:, 1]
        second = jnp.concatenate(
            [
                live_in[..., None] * v_in * low_side[:, :2],
                (live_own[:, 2, None] * v_own[:, 2] * slot_after(low_side[:, 2]))[:, None],
            ],
            axis=1,
        )
        return live_own[..., None] * v_own * high_side - second

    def partial_sums(terms):
        return jnp.sum(jnp.stack(terms), axis=(1, 2, 3))

    def precondition(res_own, res_in, c_own, c_in):
        z_own = weights[..., None] * res_own + live_own[..., None] * c_own[..., None]
        z_in = weights_in[..., None] * res_in + live_in[..., None] * c_in[..., None]
        return z_own, z_in

    start_traces, start_means = jax.vmap(setup_one)(patch_loads, transforms, inverses)
    gathered = gather_all(start_means.reshape(-1))
    res_own, res_in, received, gathered = jumps(
        start_traces, True, (extra_owner, extra_group), gathered
    )
    rows_in = jnp.stack([received[0][:, :coarse_size], received[1][:, :coarse_size]], axis=1)
    weights_in = jnp.stack([received[0][:, coarse_size], received[1][:, coarse_size]], axis=1)
    c_own, c_in = coarse(interface_means(gathered))
    dir_own, dir_in = precondition(res_own, res_in, c_own, c_in)
    traces_one = solve(dir_own, dir_in)
    parts = partial_sums([res_own * dir_own, split_terms(dir_own, dir_in, traces_one)])
    gathered = gather_all(jnp.concatenate([face_means(traces_one), parts]))
    img_own, img_in, _, _ = jumps(traces_one, True, (extra_owner[:, :0], extra_group[:, :0]))
    totals = jnp.sum(gathered[:, :, slot_count * 6 :], axis=(0, 1))
    product = totals[0:1]
    curve = totals[1:2]
    step_len = (product / curve)[:, None, None]
    cq_own, cq_in = coarse(interface_means(gathered[:, :, : slot_count * 6]))
    multiplier = step_len * dir_own
    res_own = res_own - step_len * img_own
    res_in = res_in - step_len * img_in
    z_own, z_in = precondition(
        res_own, res_in, c_own - step_len[0] * cq_own, c_in - step_len[0] * cq_in
    )

    traces_two = solve(z_own, z_in)
    parts = partial_sums(
        [
            res_own * z_own,
            z_own * img_own,
            split_terms(z_own, z_in, traces_two),
            split_terms(dir_own, dir_in, traces_two),
        ]
    )
    gathered = gather_all(parts)
    fz_own = jumps(traces_two, False)
    totals = jnp.sum(gathered, axis=(0, 1))
    new_product = totals[0:1]
    ratio = new_product / product
    curve_two = totals[2:3] + ratio * (totals[1:2] + totals[3:4]) + ratio * ratio * curve
    step_two = (new_product / curve_two)[:, None, None]
    ratio = ratio[:, None, None]
    direction = z_own + ratio * dir_own
    applied = fz_own + ratio * img_own
    multiplier = multiplier + step_two * direction
    residual = res_own - step_two * applied
    multiplier, residual = lax.optimization_barrier((multiplier, residual))
    return (multiplier[None, None], residual[None, None])


def solution(mesh):
    return jax.shard_map(
        on_device,
        mesh=mesh,
        in_specs=(
            P("grp", "dev", None, None, None),
            P("grp", "dev", None, None, None),
            P("grp", "dev", None, None),
            P("grp", "dev", None, None),
            P(),
            P("grp", "dev", None, None),
        ),
        out_specs=(P("grp", "dev", None, None, None), P("grp", "dev", None, None, None)),
        check_vma=False,
    )
```

```python
import jax
import jax.numpy as jnp
from jax import lax
from jax.sharding import PartitionSpec as P

PRECISE = lax.Precision.HIGHEST
FAST = lax.Precision.HIGH


def shifted(block, axis, distance):
    devices = range(lax.axis_size(axis))
    route = [((i - distance) % len(devices), i) for i in devices]
    return lax.ppermute(block, axis, route)


def inverse_diagonal(diagonal):
    return 1.0 / (diagonal[:, None, None] + diagonal[None, :, None] + diagonal[None, None, :])


def spectral(patch_load, transform):
    points = transform.shape[0]
    spatial = patch_load.astype(jnp.float32).reshape(points, points, points)
    moved = jnp.einsum("ai,abc->ibc", transform, spatial, precision=FAST)
    moved = jnp.einsum("bj,ibc->ijc", transform, moved, precision=FAST)
    return jnp.einsum("ck,ijc->ijk", transform, moved, precision=FAST)


def face_spectrum(transform, low_side, high_side):
    points = transform.shape[0]
    planes = jnp.stack([low_side, high_side]).reshape(2, 3, points, points)
    hats = jnp.einsum("bj,edbc,ck->edjk", transform, planes, transform, precision=FAST)
    low_row = transform[0]
    high_row = transform[points - 1]
    result = low_row[:, None, None] * hats[0, 0][None] + high_row[:, None, None] * hats[1, 0][None]
    result = (
        result
        + low_row[None, :, None] * hats[0, 1][:, None, :]
        + high_row[None, :, None] * hats[1, 1][:, None, :]
    )
    result = (
        result
        + low_row[None, None, :] * hats[0, 2][:, :, None]
        + high_row[None, None, :] * hats[1, 2][:, :, None]
    )
    return result


def trace_solved(transform, solved):
    points = transform.shape[0]
    end_rows = jnp.stack([transform[0], transform[points - 1]])
    along_a = jnp.sum(end_rows[:, :, None, None] * solved[None], axis=1)
    along_b = jnp.sum(end_rows[:, None, :, None] * solved[None], axis=2)
    along_c = jnp.sum(end_rows[:, None, None, :] * solved[None], axis=3)
    planes = jnp.stack([along_a, along_b, along_c], axis=1)
    traces = jnp.einsum("bj,edjk,ck->edbc", transform, planes, transform, precision=FAST)
    return traces.reshape(2, 3, points * points)


def plane_means(transform, solved):
    points = transform.shape[0]
    end_rows = jnp.stack([transform[0], transform[points - 1]])
    spread = jnp.mean(transform, axis=0)
    along_a = jnp.sum(end_rows[:, :, None, None] * solved[None], axis=1)
    along_b = jnp.sum(end_rows[:, None, :, None] * solved[None], axis=2)
    along_c = jnp.sum(end_rows[:, None, None, :] * solved[None], axis=3)
    planes = jnp.stack([along_a, along_b, along_c], axis=1)
    return jnp.sum(planes * spread[:, None] * spread[None, :], axis=(2, 3))


def setup_one(patch_load, one_transform, one_inverse):
    solved = one_inverse * spectral(patch_load, one_transform)
    return trace_solved(one_transform, solved), plane_means(one_transform, solved)


def apply_one(one_transform, one_inverse, low_side, high_side):
    return trace_solved(
        one_transform, one_inverse * face_spectrum(one_transform, low_side, high_side)
    )


def slot_before(vector):
    return jnp.concatenate([jnp.zeros_like(vector[:1]), vector[:-1]], axis=0)


def slot_after(vector):
    return jnp.concatenate([vector[1:], jnp.zeros_like(vector[:1])], axis=0)


def on_device(load_vector, transform, diagonal, scaling, live_count, coarse_inverse):
    patch_loads = load_vector[0, 0]
    transforms = transform[0, 0]
    diagonals = diagonal[0, 0]
    weights = scaling[0, 0]
    coarse_rows = coarse_inverse[0, 0]
    slot_count = patch_loads.shape[0]
    coarse_size = coarse_rows.shape[-1]
    group_index = lax.axis_index("grp")
    owner_index = lax.axis_index("dev")
    groups = lax.axis_size("grp")
    owners = lax.axis_size("dev")
    prev_owner = (owner_index + owners - 1) % owners
    prev_group = (group_index + groups - 1) % groups

    rows = coarse_rows.reshape(slot_count, 3, coarse_size)
    extra_owner = jnp.concatenate([rows[:, 0], weights[:, 0:1]], axis=1)
    extra_group = jnp.concatenate([rows[:, 1], weights[:, 1:2]], axis=1)

    slot_index = jnp.arange(slot_count, dtype=jnp.int32)
    in_use = slot_index[None, None, :] < live_count[:, :, None]
    nothing = jnp.zeros_like(in_use[:, :, :1])
    alive = jnp.stack(
        [
            in_use & jnp.roll(in_use, -1, axis=1),
            in_use & jnp.roll(in_use, -1, axis=0),
            in_use & jnp.concatenate([in_use[:, :, 1:], nothing], axis=2),
        ],
        axis=-1,
    ).astype(jnp.float32)
    live_own = alive[group_index, owner_index]
    live_in = jnp.stack(
        [alive[group_index, prev_owner, :, 0], alive[prev_group, owner_index, :, 1]], axis=1
    )

    inverses = jax.vmap(inverse_diagonal)(diagonals)
    solver = jax.vmap(apply_one)

    def gather_all(payload):
        count = groups * owners
        spread = jnp.broadcast_to(payload[None], (count,) + payload.shape)
        got = lax.all_to_all(spread, ("grp", "dev"), 0, 0, tiled=True)
        return got.reshape(groups, owners, -1)

    def face_means(traces):
        return jnp.mean(traces, axis=-1).reshape(-1)

    def interface_means(raw):
        raw = raw.reshape(groups, owners, slot_count, 2, 3)
        low = raw[:, :, :, 0]
        high = raw[:, :, :, 1]
        following = jnp.stack(
            [
                jnp.roll(low[..., 0], -1, axis=1),
                jnp.roll(low[..., 1], -1, axis=0),
                jnp.concatenate([low[:, :, 1:, 2], jnp.zeros_like(low[:, :, :1, 2])], axis=2),
            ],
            axis=-1,
        )
        return (alive * (high - following)).reshape(groups, coarse_size)

    def coarse(means):
        here = means[group_index]
        before = means[prev_group]
        own = jnp.dot(coarse_rows, here, precision=PRECISE).reshape(slot_count, 3)
        first = jnp.dot(rows_in[:, 0], here, precision=PRECISE)
        second = jnp.dot(rows_in[:, 1], before, precision=PRECISE)
        return own, jnp.stack([first, second], axis=1)

    def jumps(traces_now, both, extra=None, after=None):
        low_side = traces_now[:, 0]
        high_side = traces_now[:, 1]
        face_size = high_side.shape[-1]
        sends = [low_side[:, 0], low_side[:, 1]]
        if both:
            sends += [
                jnp.concatenate([high_side[:, 0], extra[0]], axis=1),
                jnp.concatenate([high_side[:, 1], extra[1]], axis=1),
            ]
        sends, after = lax.optimization_barrier((sends, after))
        low_next_owner = shifted(sends[0], "dev", -1)
        low_next_group = shifted(sends[1], "grp", -1)
        following = jnp.stack(
            [low_next_owner, low_next_group, slot_after(low_side[:, 2])], axis=1
        )
        own = live_own[..., None] * (high_side - following)
        if not both:
            return own
        high_prev_owner = shifted(sends[2], "dev", 1)
        high_prev_group = shifted(sends[3], "grp", 1)
        leading = jnp.stack(
            [high_prev_owner[:, :face_size], high_prev_group[:, :face_size]], axis=1
        )
        incoming = live_in[..., None] * (leading - low_side[:, :2])
        tail = (high_prev_owner[:, face_size:], high_prev_group[:, face_size:])
        return own, incoming, tail, after

    def solve(v_own, v_in):
        preceding = jnp.stack([v_in[:, 0], v_in[:, 1], slot_before(v_own[:, 2])], axis=1)
        return solver(transforms, inverses, -preceding, v_own)

    def split_terms(v_own, v_in, traces_now):
        low_side = traces_now[:, 0]
        high_side = traces_now[:, 1]
        second = jnp.concatenate(
            [
                live_in[..., None] * v_in * low_side[:, :2],
                (live_own[:, 2, None] * v_own[:, 2] * slot_after(low_side[:, 2]))[:, None],
            ],
            axis=1,
        )
        return live_own[..., None] * v_own * high_side - second

    def partial_sums(terms):
        return jnp.sum(jnp.stack(terms), axis=(1, 2, 3))

    def precondition(res_own, res_in, c_own, c_in):
        z_own = weights[..., None] * res_own + live_own[..., None] * c_own[..., None]
        z_in = weights_in[..., None] * res_in + live_in[..., None] * c_in[..., None]
        return z_own, z_in

    start_traces, start_means = jax.vmap(setup_one)(patch_loads, transforms, inverses)
    gathered = gather_all(start_means.reshape(-1))
    res_own, res_in, received, gathered = jumps(
        start_traces, True, (extra_owner, extra_group), gathered
    )
    rows_in = jnp.stack([received[0][:, :coarse_size], received[1][:, :coarse_size]], axis=1)
    weights_in = jnp.stack([received[0][:, coarse_size], received[1][:, coarse_size]], axis=1)
    c_own, c_in = coarse(interface_means(gathered))
    dir_own, dir_in = precondition(res_own, res_in, c_own, c_in)
    traces_one = solve(dir_own, dir_in)
    parts = partial_sums([res_own * dir_own, split_terms(dir_own, dir_in, traces_one)])
    gathered = gather_all(jnp.concatenate([face_means(traces_one), parts]))
    img_own, img_in, _, _ = jumps(traces_one, True, (extra_owner[:, :0], extra_group[:, :0]))
    totals = jnp.sum(gathered[:, :, slot_count * 6 :], axis=(0, 1))
    product = totals[0:1]
    curve = totals[1:2]
    step_len = (product / curve)[:, None, None]
    cq_own, cq_in = coarse(interface_means(gathered[:, :, : slot_count * 6]))
    multiplier = step_len * dir_own
    res_own = res_own - step_len * img_own
    res_in = res_in - step_len * img_in
    z_own, z_in = precondition(
        res_own, res_in, c_own - step_len[0] * cq_own, c_in - step_len[0] * cq_in
    )

    traces_two = solve(z_own, z_in)
    parts = partial_sums(
        [
            res_own * z_own,
            z_own * img_own,
            split_terms(z_own, z_in, traces_two),
            split_terms(dir_own, dir_in, traces_two),
        ]
    )
    gathered = gather_all(parts)
    fz_own = jumps(traces_two, False)
    totals = jnp.sum(gathered, axis=(0, 1))
    new_product = totals[0:1]
    ratio = new_product / product
    curve_two = totals[2:3] + ratio * (totals[1:2] + totals[3:4]) + ratio * ratio * curve
    step_two = (new_product / curve_two)[:, None, None]
    ratio = ratio[:, None, None]
    direction = z_own + ratio * dir_own
    applied = fz_own + ratio * img_own
    multiplier = multiplier + step_two * direction
    residual = res_own - step_two * applied
    multiplier = lax.optimization_barrier(multiplier)
    return (multiplier[None, None], residual[None, None])


def solution(mesh):
    return jax.shard_map(
        on_device,
        mesh=mesh,
        in_specs=(
            P("grp", "dev", None, None, None),
            P("grp", "dev", None, None, None),
            P("grp", "dev", None, None),
            P("grp", "dev", None, None),
            P(),
            P("grp", "dev", None, None),
        ),
        out_specs=(P("grp", "dev", None, None, None), P("grp", "dev", None, None, None)),
        check_vma=False,
    )
```

```python
import jax
import jax.numpy as jnp
from jax import lax
from jax.sharding import PartitionSpec as P

PRECISE = lax.Precision.HIGHEST
FAST = lax.Precision.HIGH


def shifted(block, axis, distance):
    devices = range(lax.axis_size(axis))
    route = [((i - distance) % len(devices), i) for i in devices]
    return lax.ppermute(block, axis, route)


def inverse_diagonal(diagonal):
    return 1.0 / (diagonal[:, None, None] + diagonal[None, :, None] + diagonal[None, None, :])


def spectral(patch_load, transform):
    points = transform.shape[0]
    spatial = patch_load.astype(jnp.float32).reshape(points, points, points)
    moved = jnp.einsum("ai,abc->ibc", transform, spatial, precision=FAST)
    moved = jnp.einsum("bj,ibc->ijc", transform, moved, precision=FAST)
    return jnp.einsum("ck,ijc->ijk", transform, moved, precision=FAST)


def face_spectrum(transform, low_side, high_side):
    points = transform.shape[0]
    planes = jnp.stack([low_side, high_side]).reshape(2, 3, points, points)
    hats = jnp.einsum("bj,edbc,ck->edjk", transform, planes, transform, precision=FAST)
    low_row = transform[0]
    high_row = transform[points - 1]
    result = low_row[:, None, None] * hats[0, 0][None] + high_row[:, None, None] * hats[1, 0][None]
    result = (
        result
        + low_row[None, :, None] * hats[0, 1][:, None, :]
        + high_row[None, :, None] * hats[1, 1][:, None, :]
    )
    result = (
        result
        + low_row[None, None, :] * hats[0, 2][:, :, None]
        + high_row[None, None, :] * hats[1, 2][:, :, None]
    )
    return result


def trace_solved(transform, solved):
    points = transform.shape[0]
    end_rows = jnp.stack([transform[0], transform[points - 1]])
    along_a = jnp.sum(end_rows[:, :, None, None] * solved[None], axis=1)
    along_b = jnp.sum(end_rows[:, None, :, None] * solved[None], axis=2)
    along_c = jnp.sum(end_rows[:, None, None, :] * solved[None], axis=3)
    planes = jnp.stack([along_a, along_b, along_c], axis=1)
    traces = jnp.einsum("bj,edjk,ck->edbc", transform, planes, transform, precision=FAST)
    return traces.reshape(2, 3, points * points)


def plane_means(transform, solved):
    points = transform.shape[0]
    end_rows = jnp.stack([transform[0], transform[points - 1]])
    spread = jnp.mean(transform, axis=0)
    along_a = jnp.sum(end_rows[:, :, None, None] * solved[None], axis=1)
    along_b = jnp.sum(end_rows[:, None, :, None] * solved[None], axis=2)
    along_c = jnp.sum(end_rows[:, None, None, :] * solved[None], axis=3)
    planes = jnp.stack([along_a, along_b, along_c], axis=1)
    return jnp.sum(planes * spread[:, None] * spread[None, :], axis=(2, 3))


def setup_one(patch_load, one_transform, one_inverse):
    solved = one_inverse * spectral(patch_load, one_transform)
    return trace_solved(one_transform, solved), plane_means(one_transform, solved)


def apply_one(one_transform, one_inverse, low_side, high_side):
    return trace_solved(
        one_transform, one_inverse * face_spectrum(one_transform, low_side, high_side)
    )


def slot_before(vector):
    return jnp.concatenate([jnp.zeros_like(vector[:1]), vector[:-1]], axis=0)


def slot_after(vector):
    return jnp.concatenate([vector[1:], jnp.zeros_like(vector[:1])], axis=0)


def on_device(load_vector, transform, diagonal, scaling, live_count, coarse_inverse):
    patch_loads = load_vector[0, 0]
    transforms = transform[0, 0]
    diagonals = diagonal[0, 0]
    weights = scaling[0, 0]
    coarse_rows = coarse_inverse[0, 0]
    slot_count = patch_loads.shape[0]
    coarse_size = coarse_rows.shape[-1]
    group_index = lax.axis_index("grp")
    owner_index = lax.axis_index("dev")
    groups = lax.axis_size("grp")
    owners = lax.axis_size("dev")
    prev_owner = (owner_index + owners - 1) % owners
    prev_group = (group_index + groups - 1) % groups

    rows = coarse_rows.reshape(slot_count, 3, coarse_size)
    extra_owner = jnp.concatenate([rows[:, 0], weights[:, 0:1]], axis=1)
    extra_group = jnp.concatenate([rows[:, 1], weights[:, 1:2]], axis=1)

    slot_index = jnp.arange(slot_count, dtype=jnp.int32)
    in_use = slot_index[None, None, :] < live_count[:, :, None]
    nothing = jnp.zeros_like(in_use[:, :, :1])
    alive = jnp.stack(
        [
            in_use & jnp.roll(in_use, -1, axis=1),
            in_use & jnp.roll(in_use, -1, axis=0),
            in_use & jnp.concatenate([in_use[:, :, 1:], nothing], axis=2),
        ],
        axis=-1,
    ).astype(jnp.float32)
    live_own = alive[group_index, owner_index]
    live_in = jnp.stack(
        [alive[group_index, prev_owner, :, 0], alive[prev_group, owner_index, :, 1]], axis=1
    )

    inverses = jax.vmap(inverse_diagonal)(diagonals)
    solver = jax.vmap(apply_one)

    def gather_all(payload):
        count = groups * owners
        spread = jnp.broadcast_to(payload[None], (count,) + payload.shape)
        got = lax.all_to_all(spread, ("grp", "dev"), 0, 0, tiled=True)
        return got.reshape(groups, owners, -1)

    def face_means(traces):
        return jnp.mean(traces, axis=-1).reshape(-1)

    def interface_means(raw):
        raw = raw.reshape(groups, owners, slot_count, 2, 3)
        low = raw[:, :, :, 0]
        high = raw[:, :, :, 1]
        following = jnp.stack(
            [
                jnp.roll(low[..., 0], -1, axis=1),
                jnp.roll(low[..., 1], -1, axis=0),
                jnp.concatenate([low[:, :, 1:, 2], jnp.zeros_like(low[:, :, :1, 2])], axis=2),
            ],
            axis=-1,
        )
        return (alive * (high - following)).reshape(groups, coarse_size)

    def coarse(means):
        here = means[group_index]
        before = means[prev_group]
        near = jnp.concatenate([coarse_rows, rows_in[:, 0]], axis=0)
        values = jnp.sum(near * here[None, :], axis=1)
        second = jnp.sum(rows_in[:, 1] * before[None, :], axis=1)
        own = values[: slot_count * 3].reshape(slot_count, 3)
        return own, jnp.stack([values[slot_count * 3 :], second], axis=1)

    def jumps(traces_now, both, extra=None, after=None):
        low_side = traces_now[:, 0]
        high_side = traces_now[:, 1]
        face_size = high_side.shape[-1]
        sends = [low_side[:, 0], low_side[:, 1]]
        if both:
            sends += [
                jnp.concatenate([high_side[:, 0], extra[0]], axis=1),
                jnp.concatenate([high_side[:, 1], extra[1]], axis=1),
            ]
        sends, after = lax.optimization_barrier((sends, after))
        low_next_owner = shifted(sends[0], "dev", -1)
        low_next_group = shifted(sends[1], "grp", -1)
        following = jnp.stack(
            [low_next_owner, low_next_group, slot_after(low_side[:, 2])], axis=1
        )
        own = live_own[..., None] * (high_side - following)
        if not both:
            return own
        high_prev_owner = shifted(sends[2], "dev", 1)
        high_prev_group = shifted(sends[3], "grp", 1)
        leading = jnp.stack(
            [high_prev_owner[:, :face_size], high_prev_group[:, :face_size]], axis=1
        )
        incoming = live_in[..., None] * (leading - low_side[:, :2])
        tail = (high_prev_owner[:, face_size:], high_prev_group[:, face_size:])
        return own, incoming, tail, after

    def solve(v_own, v_in):
        preceding = jnp.stack([v_in[:, 0], v_in[:, 1], slot_before(v_own[:, 2])], axis=1)
        return solver(transforms, inverses, -preceding, v_own)

    def split_terms(v_own, v_in, traces_now):
        low_side = traces_now[:, 0]
        high_side = traces_now[:, 1]
        second = jnp.concatenate(
            [
                live_in[..., None] * v_in * low_side[:, :2],
                (live_own[:, 2, None] * v_own[:, 2] * slot_after(low_side[:, 2]))[:, None],
            ],
            axis=1,
        )
        return live_own[..., None] * v_own * high_side - second

    def partial_sums(terms):
        return jnp.sum(jnp.stack(terms), axis=(1, 2, 3))

    def precondition(res_own, res_in, c_own, c_in):
        z_own = weights[..., None] * res_own + live_own[..., None] * c_own[..., None]
        z_in = weights_in[..., None] * res_in + live_in[..., None] * c_in[..., None]
        return z_own, z_in

    start_traces, start_means = jax.vmap(setup_one)(patch_loads, transforms, inverses)
    gathered = gather_all(start_means.reshape(-1))
    res_own, res_in, received, gathered = jumps(
        start_traces, True, (extra_owner, extra_group), gathered
    )
    rows_in = jnp.stack([received[0][:, :coarse_size], received[1][:, :coarse_size]], axis=1)
    weights_in = jnp.stack([received[0][:, coarse_size], received[1][:, coarse_size]], axis=1)
    c_own, c_in = coarse(interface_means(gathered))
    dir_own, dir_in = precondition(res_own, res_in, c_own, c_in)
    traces_one = solve(dir_own, dir_in)
    parts = partial_sums([res_own * dir_own, split_terms(dir_own, dir_in, traces_one)])
    gathered = gather_all(jnp.concatenate([face_means(traces_one), parts]))
    img_own, img_in, _, _ = jumps(traces_one, True, (extra_owner[:, :0], extra_group[:, :0]))
    totals = jnp.sum(gathered[:, :, slot_count * 6 :], axis=(0, 1))
    product = totals[0:1]
    curve = totals[1:2]
    step_len = (product / curve)[:, None, None]
    cq_own, cq_in = coarse(interface_means(gathered[:, :, : slot_count * 6]))
    multiplier = step_len * dir_own
    res_own = res_own - step_len * img_own
    res_in = res_in - step_len * img_in
    z_own, z_in = precondition(
        res_own, res_in, c_own - step_len[0] * cq_own, c_in - step_len[0] * cq_in
    )

    traces_two = solve(z_own, z_in)
    parts = partial_sums(
        [
            res_own * z_own,
            z_own * img_own,
            split_terms(z_own, z_in, traces_two),
            split_terms(dir_own, dir_in, traces_two),
        ]
    )
    gathered = gather_all(parts)
    fz_own = jumps(traces_two, False)
    totals = jnp.sum(gathered, axis=(0, 1))
    new_product = totals[0:1]
    ratio = new_product / product
    curve_two = totals[2:3] + ratio * (totals[1:2] + totals[3:4]) + ratio * ratio * curve
    step_two = (new_product / curve_two)[:, None, None]
    ratio = ratio[:, None, None]
    direction = z_own + ratio * dir_own
    applied = fz_own + ratio * img_own
    multiplier = multiplier + step_two * direction
    residual = res_own - step_two * applied
    multiplier = lax.optimization_barrier(multiplier)
    return (multiplier[None, None], residual[None, None])


def solution(mesh):
    return jax.shard_map(
        on_device,
        mesh=mesh,
        in_specs=(
            P("grp", "dev", None, None, None),
            P("grp", "dev", None, None, None),
            P("grp", "dev", None, None),
            P("grp", "dev", None, None),
            P(),
            P("grp", "dev", None, None),
        ),
        out_specs=(P("grp", "dev", None, None, None), P("grp", "dev", None, None, None)),
        check_vma=False,
    )
```

```python
import jax
import jax.numpy as jnp
from jax import lax
from jax.sharding import PartitionSpec as P

PRECISE = lax.Precision.HIGHEST
FAST = lax.Precision.HIGH


def shifted(block, axis, distance):
    devices = range(lax.axis_size(axis))
    route = [((i - distance) % len(devices), i) for i in devices]
    return lax.ppermute(block, axis, route)


def inverse_diagonal(diagonal):
    return 1.0 / (diagonal[:, None, None] + diagonal[None, :, None] + diagonal[None, None, :])


def spectral(patch_load, transform):
    points = transform.shape[0]
    spatial = patch_load.astype(jnp.float32).reshape(points, points, points)
    moved = jnp.einsum("ai,abc->ibc", transform, spatial, precision=FAST)
    moved = jnp.einsum("bj,ibc->ijc", transform, moved, precision=FAST)
    return jnp.einsum("ck,ijc->ijk", transform, moved, precision=FAST)


def face_spectrum(transform, low_side, high_side):
    points = transform.shape[0]
    planes = jnp.stack([low_side, high_side]).reshape(2, 3, points, points)
    hats = jnp.einsum("bj,edbc,ck->edjk", transform, planes, transform, precision=FAST)
    low_row = transform[0]
    high_row = transform[points - 1]
    result = low_row[:, None, None] * hats[0, 0][None] + high_row[:, None, None] * hats[1, 0][None]
    result = (
        result
        + low_row[None, :, None] * hats[0, 1][:, None, :]
        + high_row[None, :, None] * hats[1, 1][:, None, :]
    )
    result = (
        result
        + low_row[None, None, :] * hats[0, 2][:, :, None]
        + high_row[None, None, :] * hats[1, 2][:, :, None]
    )
    return result


def trace_solved(transform, solved):
    points = transform.shape[0]
    end_rows = jnp.stack([transform[0], transform[points - 1]])
    along_a = jnp.sum(end_rows[:, :, None, None] * solved[None], axis=1)
    along_b = jnp.sum(end_rows[:, None, :, None] * solved[None], axis=2)
    along_c = jnp.sum(end_rows[:, None, None, :] * solved[None], axis=3)
    planes = jnp.stack([along_a, along_b, along_c], axis=1)
    traces = jnp.einsum("bj,edjk,ck->edbc", transform, planes, transform, precision=FAST)
    return traces.reshape(2, 3, points * points)


def plane_means(transform, solved):
    points = transform.shape[0]
    end_rows = jnp.stack([transform[0], transform[points - 1]])
    spread = jnp.mean(transform, axis=0)
    along_a = jnp.sum(end_rows[:, :, None, None] * solved[None], axis=1)
    along_b = jnp.sum(end_rows[:, None, :, None] * solved[None], axis=2)
    along_c = jnp.sum(end_rows[:, None, None, :] * solved[None], axis=3)
    planes = jnp.stack([along_a, along_b, along_c], axis=1)
    return jnp.sum(planes * spread[:, None] * spread[None, :], axis=(2, 3))


def setup_one(patch_load, one_transform, one_inverse):
    solved = one_inverse * spectral(patch_load, one_transform)
    return trace_solved(one_transform, solved), plane_means(one_transform, solved)


def apply_one(one_transform, one_inverse, low_side, high_side):
    return trace_solved(
        one_transform, one_inverse * face_spectrum(one_transform, low_side, high_side)
    )


def slot_before(vector):
    return jnp.concatenate([jnp.zeros_like(vector[:1]), vector[:-1]], axis=0)


def slot_after(vector):
    return jnp.concatenate([vector[1:], jnp.zeros_like(vector[:1])], axis=0)


def on_device(load_vector, transform, diagonal, scaling, live_count, coarse_inverse):
    patch_loads = load_vector[0, 0]
    transforms = transform[0, 0]
    diagonals = diagonal[0, 0]
    weights = scaling[0, 0]
    coarse_rows = coarse_inverse[0, 0]
    slot_count = patch_loads.shape[0]
    coarse_size = coarse_rows.shape[-1]
    group_index = lax.axis_index("grp")
    owner_index = lax.axis_index("dev")
    groups = lax.axis_size("grp")
    owners = lax.axis_size("dev")
    prev_owner = (owner_index + owners - 1) % owners
    prev_group = (group_index + groups - 1) % groups

    rows = coarse_rows.reshape(slot_count, 3, coarse_size)
    extra_owner = jnp.concatenate([rows[:, 0], weights[:, 0:1]], axis=1)
    extra_group = jnp.concatenate([rows[:, 1], weights[:, 1:2]], axis=1)

    slot_index = jnp.arange(slot_count, dtype=jnp.int32)
    in_use = slot_index[None, None, :] < live_count[:, :, None]
    nothing = jnp.zeros_like(in_use[:, :, :1])
    alive = jnp.stack(
        [
            in_use & jnp.roll(in_use, -1, axis=1),
            in_use & jnp.roll(in_use, -1, axis=0),
            in_use & jnp.concatenate([in_use[:, :, 1:], nothing], axis=2),
        ],
        axis=-1,
    ).astype(jnp.float32)
    live_own = alive[group_index, owner_index]
    live_in = jnp.stack(
        [alive[group_index, prev_owner, :, 0], alive[prev_group, owner_index, :, 1]], axis=1
    )

    inverses = jax.vmap(inverse_diagonal)(diagonals)
    solver = jax.vmap(apply_one)

    def gather_all(payload):
        count = groups * owners
        spread = jnp.broadcast_to(payload[None], (count,) + payload.shape)
        got = lax.all_to_all(spread, ("grp", "dev"), 0, 0, tiled=True)
        return got.reshape(groups, owners, -1)

    def face_means(traces):
        return jnp.mean(traces, axis=-1).reshape(-1)

    def interface_means(raw):
        raw = raw.reshape(groups, owners, slot_count, 2, 3)
        low = raw[:, :, :, 0]
        high = raw[:, :, :, 1]
        following = jnp.stack(
            [
                jnp.roll(low[..., 0], -1, axis=1),
                jnp.roll(low[..., 1], -1, axis=0),
                jnp.concatenate([low[:, :, 1:, 2], jnp.zeros_like(low[:, :, :1, 2])], axis=2),
            ],
            axis=-1,
        )
        return (alive * (high - following)).reshape(groups, coarse_size)

    def coarse(means):
        here = means[group_index]
        before = means[prev_group]
        own = jnp.dot(coarse_rows, here, precision=PRECISE).reshape(slot_count, 3)
        first = jnp.dot(rows_in[:, 0], here, precision=PRECISE)
        second = jnp.dot(rows_in[:, 1], before, precision=PRECISE)
        return own, jnp.stack([first, second], axis=1)

    def jumps(traces_now, both, extra=None, after=None):
        low_side = traces_now[:, 0]
        high_side = traces_now[:, 1]
        face_size = high_side.shape[-1]
        sends = [low_side[:, 0], low_side[:, 1]]
        if both:
            sends += [
                jnp.concatenate([high_side[:, 0], extra[0]], axis=1),
                jnp.concatenate([high_side[:, 1], extra[1]], axis=1),
            ]
        if both and after is not None:
            lows = lax.optimization_barrier(sends[:2])
            highs, after = lax.optimization_barrier((sends[2:], after))
            sends = list(lows) + list(highs)
        else:
            sends, after = lax.optimization_barrier((sends, after))
        low_next_owner = shifted(sends[0], "dev", -1)
        low_next_group = shifted(sends[1], "grp", -1)
        following = jnp.stack(
            [low_next_owner, low_next_group, slot_after(low_side[:, 2])], axis=1
        )
        own = live_own[..., None] * (high_side - following)
        if not both:
            return own
        high_prev_owner = shifted(sends[2], "dev", 1)
        high_prev_group = shifted(sends[3], "grp", 1)
        leading = jnp.stack(
            [high_prev_owner[:, :face_size], high_prev_group[:, :face_size]], axis=1
        )
        incoming = live_in[..., None] * (leading - low_side[:, :2])
        tail = (high_prev_owner[:, face_size:], high_prev_group[:, face_size:])
        return own, incoming, tail, after

    def solve(v_own, v_in):
        preceding = jnp.stack([v_in[:, 0], v_in[:, 1], slot_before(v_own[:, 2])], axis=1)
        return solver(transforms, inverses, -preceding, v_own)

    def split_terms(v_own, v_in, traces_now):
        low_side = traces_now[:, 0]
        high_side = traces_now[:, 1]
        second = jnp.concatenate(
            [
                live_in[..., None] * v_in * low_side[:, :2],
                (live_own[:, 2, None] * v_own[:, 2] * slot_after(low_side[:, 2]))[:, None],
            ],
            axis=1,
        )
        return live_own[..., None] * v_own * high_side - second

    def partial_sums(terms):
        return jnp.sum(jnp.stack(terms), axis=(1, 2, 3))

    def precondition(res_own, res_in, c_own, c_in):
        z_own = weights[..., None] * res_own + live_own[..., None] * c_own[..., None]
        z_in = weights_in[..., None] * res_in + live_in[..., None] * c_in[..., None]
        return z_own, z_in

    start_traces, start_means = jax.vmap(setup_one)(patch_loads, transforms, inverses)
    gathered = gather_all(start_means.reshape(-1))
    res_own, res_in, received, gathered = jumps(
        start_traces, True, (extra_owner, extra_group), gathered
    )
    rows_in = jnp.stack([received[0][:, :coarse_size], received[1][:, :coarse_size]], axis=1)
    weights_in = jnp.stack([received[0][:, coarse_size], received[1][:, coarse_size]], axis=1)
    c_own, c_in = coarse(interface_means(gathered))
    dir_own, dir_in = precondition(res_own, res_in, c_own, c_in)
    traces_one = solve(dir_own, dir_in)
    parts = partial_sums([res_own * dir_own, split_terms(dir_own, dir_in, traces_one)])
    gathered = gather_all(jnp.concatenate([face_means(traces_one), parts]))
    img_own, img_in, _, _ = jumps(traces_one, True, (extra_owner[:, :0], extra_group[:, :0]))
    totals = jnp.sum(gathered[:, :, slot_count * 6 :], axis=(0, 1))
    product = totals[0:1]
    curve = totals[1:2]
    step_len = (product / curve)[:, None, None]
    cq_own, cq_in = coarse(interface_means(gathered[:, :, : slot_count * 6]))
    multiplier = step_len * dir_own
    res_own = res_own - step_len * img_own
    res_in = res_in - step_len * img_in
    z_own, z_in = precondition(
        res_own, res_in, c_own - step_len[0] * cq_own, c_in - step_len[0] * cq_in
    )

    traces_two = solve(z_own, z_in)
    parts = partial_sums(
        [
            res_own * z_own,
            z_own * img_own,
            split_terms(z_own, z_in, traces_two),
            split_terms(dir_own, dir_in, traces_two),
        ]
    )
    gathered = gather_all(parts)
    fz_own = jumps(traces_two, False)
    totals = jnp.sum(gathered, axis=(0, 1))
    new_product = totals[0:1]
    ratio = new_product / product
    curve_two = totals[2:3] + ratio * (totals[1:2] + totals[3:4]) + ratio * ratio * curve
    step_two = (new_product / curve_two)[:, None, None]
    ratio = ratio[:, None, None]
    direction = z_own + ratio * dir_own
    applied = fz_own + ratio * img_own
    multiplier = multiplier + step_two * direction
    residual = res_own - step_two * applied
    multiplier = lax.optimization_barrier(multiplier)
    return (multiplier[None, None], residual[None, None])


def solution(mesh):
    return jax.shard_map(
        on_device,
        mesh=mesh,
        in_specs=(
            P("grp", "dev", None, None, None),
            P("grp", "dev", None, None, None),
            P("grp", "dev", None, None),
            P("grp", "dev", None, None),
            P(),
            P("grp", "dev", None, None),
        ),
        out_specs=(P("grp", "dev", None, None, None), P("grp", "dev", None, None, None)),
        check_vma=False,
    )
```

```python
import jax
import jax.numpy as jnp
from jax import lax
from jax.sharding import PartitionSpec as P

PRECISE = lax.Precision.HIGHEST
FAST = lax.Precision.HIGH


def shifted(block, axis, distance):
    devices = range(lax.axis_size(axis))
    route = [((i - distance) % len(devices), i) for i in devices]
    return lax.ppermute(block, axis, route)


def inverse_diagonal(diagonal):
    return 1.0 / (diagonal[:, None, None] + diagonal[None, :, None] + diagonal[None, None, :])


def spectral(patch_load, transform):
    points = transform.shape[0]
    spatial = patch_load.astype(jnp.float32).reshape(points, points, points)
    moved = jnp.einsum("ai,abc->ibc", transform, spatial, precision=FAST)
    moved = jnp.einsum("bj,ibc->ijc", transform, moved, precision=FAST)
    return jnp.einsum("ck,ijc->ijk", transform, moved, precision=FAST)


def face_spectrum(transform, low_side, high_side):
    points = transform.shape[0]
    planes = jnp.stack([low_side, high_side]).reshape(2, 3, points, points)
    hats = jnp.einsum("bj,edbc,ck->edjk", transform, planes, transform, precision=FAST)
    low_row = transform[0]
    high_row = transform[points - 1]
    result = low_row[:, None, None] * hats[0, 0][None] + high_row[:, None, None] * hats[1, 0][None]
    result = (
        result
        + low_row[None, :, None] * hats[0, 1][:, None, :]
        + high_row[None, :, None] * hats[1, 1][:, None, :]
    )
    result = (
        result
        + low_row[None, None, :] * hats[0, 2][:, :, None]
        + high_row[None, None, :] * hats[1, 2][:, :, None]
    )
    return result


def trace_solved(transform, solved):
    points = transform.shape[0]
    end_rows = jnp.stack([transform[0], transform[points - 1]])
    along_a = jnp.sum(end_rows[:, :, None, None] * solved[None], axis=1)
    along_b = jnp.sum(end_rows[:, None, :, None] * solved[None], axis=2)
    along_c = jnp.sum(end_rows[:, None, None, :] * solved[None], axis=3)
    planes = jnp.stack([along_a, along_b, along_c], axis=1)
    traces = jnp.einsum("bj,edjk,ck->edbc", transform, planes, transform, precision=FAST)
    return traces.reshape(2, 3, points * points)


def plane_means(transform, solved):
    points = transform.shape[0]
    end_rows = jnp.stack([transform[0], transform[points - 1]])
    spread = jnp.mean(transform, axis=0)
    along_a = jnp.sum(end_rows[:, :, None, None] * solved[None], axis=1)
    along_b = jnp.sum(end_rows[:, None, :, None] * solved[None], axis=2)
    along_c = jnp.sum(end_rows[:, None, None, :] * solved[None], axis=3)
    planes = jnp.stack([along_a, along_b, along_c], axis=1)
    return jnp.sum(planes * spread[:, None] * spread[None, :], axis=(2, 3))


def setup_one(patch_load, one_transform, one_inverse):
    solved = one_inverse * spectral(patch_load, one_transform)
    return trace_solved(one_transform, solved), plane_means(one_transform, solved)


def apply_one(one_transform, one_inverse, low_side, high_side):
    return trace_solved(
        one_transform, one_inverse * face_spectrum(one_transform, low_side, high_side)
    )


def slot_before(vector):
    return jnp.concatenate([jnp.zeros_like(vector[:1]), vector[:-1]], axis=0)


def slot_after(vector):
    return jnp.concatenate([vector[1:], jnp.zeros_like(vector[:1])], axis=0)


def on_device(load_vector, transform, diagonal, scaling, live_count, coarse_inverse):
    patch_loads = load_vector[0, 0]
    transforms = transform[0, 0]
    diagonals = diagonal[0, 0]
    weights = scaling[0, 0]
    coarse_rows = coarse_inverse[0, 0]
    slot_count = patch_loads.shape[0]
    coarse_size = coarse_rows.shape[-1]
    group_index = lax.axis_index("grp")
    owner_index = lax.axis_index("dev")
    groups = lax.axis_size("grp")
    owners = lax.axis_size("dev")
    prev_owner = (owner_index + owners - 1) % owners
    prev_group = (group_index + groups - 1) % groups

    rows = coarse_rows.reshape(slot_count, 3, coarse_size)
    extra_owner = jnp.concatenate([rows[:, 0], weights[:, 0:1]], axis=1)
    extra_group = jnp.concatenate([rows[:, 1], weights[:, 1:2]], axis=1)

    slot_index = jnp.arange(slot_count, dtype=jnp.int32)
    in_use = slot_index[None, None, :] < live_count[:, :, None]
    nothing = jnp.zeros_like(in_use[:, :, :1])
    alive = jnp.stack(
        [
            in_use & jnp.roll(in_use, -1, axis=1),
            in_use & jnp.roll(in_use, -1, axis=0),
            in_use & jnp.concatenate([in_use[:, :, 1:], nothing], axis=2),
        ],
        axis=-1,
    ).astype(jnp.float32)
    live_own = alive[group_index, owner_index]
    live_in = jnp.stack(
        [alive[group_index, prev_owner, :, 0], alive[prev_group, owner_index, :, 1]], axis=1
    )

    inverses = jax.vmap(inverse_diagonal)(diagonals)
    solver = jax.vmap(apply_one)

    def gather_all(payload):
        count = groups * owners
        spread = jnp.broadcast_to(payload[None], (count,) + payload.shape)
        got = lax.all_to_all(spread, ("grp", "dev"), 0, 0, tiled=True)
        return got.reshape(groups, owners, -1)

    def face_means(traces):
        return jnp.mean(traces, axis=-1).reshape(-1)

    def interface_means(raw):
        raw = raw.reshape(groups, owners, slot_count, 2, 3)
        low = raw[:, :, :, 0]
        high = raw[:, :, :, 1]
        following = jnp.stack(
            [
                jnp.roll(low[..., 0], -1, axis=1),
                jnp.roll(low[..., 1], -1, axis=0),
                jnp.concatenate([low[:, :, 1:, 2], jnp.zeros_like(low[:, :, :1, 2])], axis=2),
            ],
            axis=-1,
        )
        return (alive * (high - following)).reshape(groups, coarse_size)

    def coarse(means):
        here = means[group_index]
        before = means[prev_group]
        own = jnp.dot(coarse_rows, here, precision=FAST).reshape(slot_count, 3)
        first = jnp.dot(rows_in[:, 0], here, precision=FAST)
        second = jnp.dot(rows_in[:, 1], before, precision=FAST)
        return own, jnp.stack([first, second], axis=1)

    def jumps(traces_now, both, extra=None, after=None):
        low_side = traces_now[:, 0]
        high_side = traces_now[:, 1]
        face_size = high_side.shape[-1]
        sends = [low_side[:, 0], low_side[:, 1]]
        if both:
            sends += [
                jnp.concatenate([high_side[:, 0], extra[0]], axis=1),
                jnp.concatenate([high_side[:, 1], extra[1]], axis=1),
            ]
        sends, after = lax.optimization_barrier((sends, after))
        low_next_owner = shifted(sends[0], "dev", -1)
        low_next_group = shifted(sends[1], "grp", -1)
        following = jnp.stack(
            [low_next_owner, low_next_group, slot_after(low_side[:, 2])], axis=1
        )
        own = live_own[..., None] * (high_side - following)
        if not both:
            return own
        high_prev_owner = shifted(sends[2], "dev", 1)
        high_prev_group = shifted(sends[3], "grp", 1)
        leading = jnp.stack(
            [high_prev_owner[:, :face_size], high_prev_group[:, :face_size]], axis=1
        )
        incoming = live_in[..., None] * (leading - low_side[:, :2])
        tail = (high_prev_owner[:, face_size:], high_prev_group[:, face_size:])
        return own, incoming, tail, after

    def solve(v_own, v_in):
        preceding = jnp.stack([v_in[:, 0], v_in[:, 1], slot_before(v_own[:, 2])], axis=1)
        return solver(transforms, inverses, -preceding, v_own)

    def split_terms(v_own, v_in, traces_now):
        low_side = traces_now[:, 0]
        high_side = traces_now[:, 1]
        second = jnp.concatenate(
            [
                live_in[..., None] * v_in * low_side[:, :2],
                (live_own[:, 2, None] * v_own[:, 2] * slot_after(low_side[:, 2]))[:, None],
            ],
            axis=1,
        )
        return live_own[..., None] * v_own * high_side - second

    def partial_sums(terms):
        return jnp.sum(jnp.stack(terms), axis=(1, 2, 3))

    def precondition(res_own, res_in, c_own, c_in):
        z_own = weights[..., None] * res_own + live_own[..., None] * c_own[..., None]
        z_in = weights_in[..., None] * res_in + live_in[..., None] * c_in[..., None]
        return z_own, z_in

    start_traces, start_means = jax.vmap(setup_one)(patch_loads, transforms, inverses)
    gathered = gather_all(start_means.reshape(-1))
    res_own, res_in, received, gathered = jumps(
        start_traces, True, (extra_owner, extra_group), gathered
    )
    rows_in = jnp.stack([received[0][:, :coarse_size], received[1][:, :coarse_size]], axis=1)
    weights_in = jnp.stack([received[0][:, coarse_size], received[1][:, coarse_size]], axis=1)
    c_own, c_in = coarse(interface_means(gathered))
    dir_own, dir_in = precondition(res_own, res_in, c_own, c_in)
    traces_one = solve(dir_own, dir_in)
    parts = partial_sums([res_own * dir_own, split_terms(dir_own, dir_in, traces_one)])
    gathered = gather_all(jnp.concatenate([face_means(traces_one), parts]))
    img_own, img_in, _, _ = jumps(traces_one, True, (extra_owner[:, :0], extra_group[:, :0]))
    totals = jnp.sum(gathered[:, :, slot_count * 6 :], axis=(0, 1))
    product = totals[0:1]
    curve = totals[1:2]
    step_len = (product / curve)[:, None, None]
    cq_own, cq_in = coarse(interface_means(gathered[:, :, : slot_count * 6]))
    multiplier = step_len * dir_own
    res_own = res_own - step_len * img_own
    res_in = res_in - step_len * img_in
    z_own, z_in = precondition(
        res_own, res_in, c_own - step_len[0] * cq_own, c_in - step_len[0] * cq_in
    )

    traces_two = solve(z_own, z_in)
    parts = partial_sums(
        [
            res_own * z_own,
            z_own * img_own,
            split_terms(z_own, z_in, traces_two),
            split_terms(dir_own, dir_in, traces_two),
        ]
    )
    gathered = gather_all(parts)
    fz_own = jumps(traces_two, False)
    totals = jnp.sum(gathered, axis=(0, 1))
    new_product = totals[0:1]
    ratio = new_product / product
    curve_two = totals[2:3] + ratio * (totals[1:2] + totals[3:4]) + ratio * ratio * curve
    step_two = (new_product / curve_two)[:, None, None]
    ratio = ratio[:, None, None]
    direction = z_own + ratio * dir_own
    applied = fz_own + ratio * img_own
    multiplier = multiplier + step_two * direction
    residual = res_own - step_two * applied
    multiplier = lax.optimization_barrier(multiplier)
    return (multiplier[None, None], residual[None, None])


def solution(mesh):
    return jax.shard_map(
        on_device,
        mesh=mesh,
        in_specs=(
            P("grp", "dev", None, None, None),
            P("grp", "dev", None, None, None),
            P("grp", "dev", None, None),
            P("grp", "dev", None, None),
            P(),
            P("grp", "dev", None, None),
        ),
        out_specs=(P("grp", "dev", None, None, None), P("grp", "dev", None, None, None)),
        check_vma=False,
    )
```
